256 devices in a mesh: seq: 32 (over z, y_lo, core), mp: 8 (over y_hi, x).
Axes of the slice: x: 4, y: 4 (y_hi: 2, y_lo: 2; y = y_hi * 2 + y_lo), z: 8, core: 2. Of those that a mesh axis runs over, the one named last changes fastest.
Arguments:
- tokens: bfloat16 [12288, 3072], P('seq', 'mp'), may hold values from -6 to 6
- w_qkv: bfloat16 [3072, 3, 3072], P(None, None, 'mp'), may hold values from -1 to 1
- q_gain: float32 [128], replicated, may hold values from 0 to 5
- k_gain: float32 [128], replicated, may hold values from 0 to 5
- w_out: bfloat16 [3072, 3072], P('mp'), may hold values from -0.15625 to 0.15625
- neighbours: int32 [32, 6], replicated, may hold values from 0 to 31, as said below
- counts: int32 [32], replicated, may hold values from 1 to 6
Outputs:
- mixed: bfloat16 [12288, 3072], P('seq', 'mp')
The draws below stay inside these ranges and needn't reach their ends.
Inputs may be any that keep to these rules, and one draw needn't show every extreme that they name: `neighbours`: each row lists distinct tiles, each within 4 tiles of the row's own tile counted cyclically modulo 32.
All inputs are finite; a program needn't handle non-finite values.
Results may differ from the reference program's by a relative error of at most 0.014.
Values may be sent and summed in bfloat16 or wider, within the bound.
No kernel may reach another device: no remote copies, remote signals or barrier semaphores. Data moves between devices by JAX's collectives and lax.ppermute only.
A program may use at most 128 MiB of HBM per device.

```python
import math
import jax
import jax.numpy as jnp
from jax import lax

D = 3072
HEADS = 24
HD = 128
TILE = 384
REACH = 4
NB = 6
TILES = 32
TOKENS = 12288
H_DEV = 3


def draw_w_qkv(key, part):
    first_key = jax.random.fold_in(jax.random.fold_in(key, 11), 0)
    base = jax.random.truncated_normal(first_key, -5.0, 5.0, (D, 3, HEADS * HD), jnp.float32) / math.sqrt(D)
    return base.astype(jnp.bfloat16)


def gain_draw(key, salt):
    inner = jax.random.fold_in(key, salt)
    return jnp.exp(jax.random.uniform(inner, (HD,), jnp.float32, math.log(0.6), math.log(1.6)))


def draw_q_gain(key, part):
    return gain_draw(key, 21)


def draw_k_gain(key, part):
    return gain_draw(key, 22)


def draw_neighbours(key, part):
    breadth = 2 * REACH + 1
    ranking = jax.random.randint(jax.random.fold_in(key, 31), (TILES, breadth), 0, 1 << 20) * 32 + jnp.arange(breadth, dtype=jnp.int32)
    picked = jnp.argsort(ranking, axis=1)[:, :NB].astype(jnp.int32) - REACH
    pinned = [-REACH, REACH, -1, 1] + [value for value in range(-REACH + 1, REACH) if value not in (-1, 0, 1)] + [0]
    picked = picked.at[0].set(jnp.array(pinned[:NB], dtype=jnp.int32))
    return ((jnp.arange(TILES, dtype=jnp.int32)[:, None] + picked) % TILES).astype(jnp.int32)


def draw_counts(key, part):
    drawn = jax.random.randint(jax.random.fold_in(key, 41), (TILES,), 1, NB + 1).astype(jnp.int32)
    return drawn.at[0].set(NB).at[1].set(1)


def spiked(entries, rng, source, target, parts, factor):
    def block_of(dim):
        return (jnp.arange(entries.shape[dim]) // (entries.shape[dim] // parts)).reshape((-1,) + (1,) * (entries.ndim - 1 - dim))

    near = jax.random.permutation(rng, parts)[block_of(target)]
    second = (block_of(target) + parts // 2) % parts
    return jnp.where((block_of(source) == near) | (block_of(source) == second), factor * entries, entries)


def shard_levels(rng, dims, cuts, least, top_value):
    gain = 1.0
    for position, shards_of in cuts:
        draws = jax.random.uniform(jax.random.fold_in(jax.random.fold_in(rng, 6), position), (shards_of,), jnp.float32, least / len(cuts), top_value / len(cuts))
        gain = gain * jnp.repeat(jnp.exp(draws), dims[position] // shards_of).reshape((-1,) + (1,) * (len(dims) - 1 - position))
    return gain


def normal_values(stream_key, dims, spread, limit, shards=(), kind=jnp.bfloat16):
    entries = jax.random.normal(stream_key, dims, jnp.float32) * spread
    if len(shards) > 0:
        entries = shard_levels(stream_key, dims, shards, -0.22, 0.18) * entries
    return jnp.clip(entries, min=-limit, max=limit).astype(kind)


def bell_draw_with(stream_key, dims, deviation, reach, pieces, heavy, kind=jnp.bfloat16):
    values = deviation * jax.random.normal(stream_key, dims, jnp.float32)
    if pieces:
        values = values * shard_levels(stream_key, dims, pieces, -0.22, 0.18)
    return jnp.clip(spiked(values, jax.random.fold_in(stream_key, 3), *heavy), -reach, reach).astype(kind)


def setup_inputs(seed: int = 0) -> dict:
    keys = jax.random.split(jax.random.key(seed), 8)
    tokens = normal_values(keys[0], (TOKENS, D), 1.0, 6.0, ((0, 32), (1, 8)))
    w_qkv = draw_w_qkv(jax.random.fold_in(keys[7], 71), 0)
    q_gain = draw_q_gain(jax.random.fold_in(keys[7], 71), 0)
    k_gain = draw_k_gain(jax.random.fold_in(keys[7], 71), 0)
    w_out = bell_draw_with(keys[4], (HEADS * HD, D), (HEADS * HD) ** -0.5, 0.15625, ((0, 8),), (0, 1, 8, 2.0))
    neighbours = draw_neighbours(jax.random.fold_in(keys[7], 71), 0)
    counts = draw_counts(jax.random.fold_in(keys[7], 71), 0)
    return {"tokens": tokens, "w_qkv": w_qkv, "q_gain": q_gain, "k_gain": k_gain, "w_out": w_out, "neighbours": neighbours, "counts": counts}


def head_norm(projected, gain_vec):
    per_head = projected.reshape(projected.shape[0], HEADS, HD)
    factor = lax.rsqrt(lax.optimization_barrier(jnp.mean(per_head * per_head, axis=-1, keepdims=True)) + 1e-06)
    return (per_head * factor * gain_vec).astype(jnp.bfloat16)

def reference(tokens, w_qkv, q_gain, k_gain, w_out, neighbours, counts):
    queries = head_norm(jnp.dot(tokens, w_qkv[:, 0, :], preferred_element_type=jnp.float32), q_gain)
    key_rows = head_norm(jnp.dot(tokens, w_qkv[:, 1, :], preferred_element_type=jnp.float32), k_gain)
    value_rows = jnp.dot(tokens, w_qkv[:, 2, :], preferred_element_type=jnp.float32).astype(jnp.bfloat16)
    queries = lax.optimization_barrier(queries)
    key_rows = lax.optimization_barrier(key_rows)
    value_rows = lax.optimization_barrier(value_rows)
    query_tiles = queries.reshape(TILES, TILE, HEADS, HD)
    key_tiles = key_rows.reshape(TILES, TILE, HEADS, HD)
    value_tiles = value_rows.reshape(TILES, TILE, HEADS, HD)
    factor = HD ** (-0.5)

    def one_tile(index):
        query_block = query_tiles[index].astype(jnp.float32)
        listed = neighbours[index]
        near_keys = key_tiles[listed].reshape(NB * TILE, HEADS, HD).astype(jnp.float32)
        near_values = value_tiles[listed].reshape(NB * TILE, HEADS, HD).astype(jnp.float32)
        usable = jnp.repeat(jnp.arange(NB, dtype=jnp.int32) < counts[index], TILE)
        scores = jnp.einsum('qhd,khd->hqk', query_block, near_keys) * factor
        scores = jnp.where(usable[None, None, :], scores, -jnp.inf)
        highest = lax.optimization_barrier(jnp.max(scores, axis=-1, keepdims=True))
        expo = jnp.exp(scores - highest)
        probs = (expo / lax.optimization_barrier(jnp.sum(expo, axis=-1, keepdims=True))).astype(jnp.bfloat16)
        probs = lax.optimization_barrier(probs)
        result = jnp.einsum('hqk,khd->qhd', probs.astype(jnp.float32), near_values)
        return result.astype(jnp.bfloat16)
    attended = lax.map(one_tile, jnp.arange(TILES, dtype=jnp.int32)).reshape(TOKENS, HEADS * HD)
    summed = jnp.zeros((TOKENS, D), jnp.float32)
    group_cols = H_DEV * HD
    for group in range(HEADS // H_DEV):
        lower = group * group_cols
        term = jnp.dot(attended[:, lower:lower + group_cols], w_out[lower:lower + group_cols], preferred_element_type=jnp.float32).astype(jnp.bfloat16)
        term = lax.optimization_barrier(term)
        summed = summed + term.astype(jnp.float32)
    return summed.astype(jnp.bfloat16)
```

```python
import jax
import jax.numpy as jnp
from jax import lax
from jax.sharding import PartitionSpec as P

HD = 128
TILE = 384
REACH = 4
NB = 6


def passed_along(value, axis, steps):
    count = lax.axis_size(axis)
    pairs = [(source, (source + steps) % count) for source in range(count)]
    return lax.ppermute(value, axis, pairs)


def head_norm(projected, gain_vec):
    per_head = projected.reshape(projected.shape[0], -1, HD)
    factor = lax.rsqrt(jnp.mean(per_head * per_head, axis=-1, keepdims=True) + 1e-06)
    return (per_head * factor * gain_vec).astype(jnp.bfloat16)


def on_device(tokens, w_qkv, q_gain, k_gain, w_out, neighbours, counts):
    tok_rows = tokens.shape[0]
    columns = w_qkv.shape[2]
    heads_here = columns // HD
    tiles_here = tok_rows // TILE
    total_tiles = neighbours.shape[0]
    span_here = (REACH + tiles_here - 1) // tiles_here
    flat_w = w_qkv.reshape(w_qkv.shape[0], 3 * columns)
    feats = tokens.shape[1]
    mp_count = lax.axis_size("mp")
    mp_here = lax.axis_index("mp")
    projected = jnp.dot(
        tokens,
        lax.dynamic_slice_in_dim(flat_w, mp_here * feats, feats, 0),
        preferred_element_type=jnp.float32,
    )
    for step in range(1, mp_count):
        source = (mp_here - step) % mp_count
        projected = projected + jnp.dot(
            passed_along(tokens, "mp", step),
            lax.dynamic_slice_in_dim(flat_w, source * feats, feats, 0),
            preferred_element_type=jnp.float32,
        )
    queries = head_norm(projected[:, :columns], q_gain)
    key_part = head_norm(projected[:, columns : 2 * columns], k_gain).reshape(tok_rows, columns)
    value_part = projected[:, 2 * columns :].astype(jnp.bfloat16)
    paired = jnp.stack([key_part, value_part])
    blocks = []
    for offset in range(-span_here, span_here + 1):
        if offset == 0:
            blocks.append(paired)
        else:
            blocks.append(passed_along(paired, "seq", -offset))
    window = jnp.concatenate(blocks, axis=1)
    window_tiles = (2 * span_here + 1) * tiles_here
    position = lax.axis_index("seq")
    first_tile = position * tiles_here - span_here * tiles_here
    listed = lax.dynamic_slice_in_dim(neighbours, position * tiles_here, tiles_here, 0)
    used_counts = lax.dynamic_slice_in_dim(counts, position * tiles_here, tiles_here, 0)
    relative = jnp.mod(listed - first_tile, total_tiles)
    slot_used = jnp.arange(NB, dtype=jnp.int32)[None, :] < used_counts[:, None]
    query_blocks = queries.reshape(tiles_here, TILE, heads_here, HD)
    factor = HD ** (-0.5)
    hits = (
        relative[:, :, None] == jnp.arange(window_tiles, dtype=jnp.int32)[None, None, :]
    ) & slot_used[:, :, None]
    tile_mask = jnp.any(hits, axis=1)
    key_mask = jnp.repeat(tile_mask, TILE, axis=1)
    near_keys = window[0].reshape(window_tiles * TILE, heads_here, HD)
    near_values = window[1].reshape(window_tiles * TILE, heads_here, HD)
    scores = (
        jnp.einsum("tqhd,khd->thqk", query_blocks, near_keys, preferred_element_type=jnp.float32)
        * factor
    )
    scores = jnp.where(key_mask[:, None, None, :], scores, -jnp.inf)
    highest = jnp.max(scores, axis=-1, keepdims=True)
    expo = jnp.exp(scores - highest)
    probs = (expo / jnp.sum(expo, axis=-1, keepdims=True)).astype(jnp.bfloat16)
    attended = jnp.einsum("thqk,khd->tqhd", probs, near_values, preferred_element_type=jnp.float32)
    attended = attended.astype(jnp.bfloat16).reshape(tok_rows, columns)
    out_cols = w_out.shape[1] // mp_count
    total = jnp.dot(
        attended,
        lax.dynamic_slice_in_dim(w_out, mp_here * out_cols, out_cols, 1),
        preferred_element_type=jnp.float32,
    ).astype(jnp.bfloat16).astype(jnp.float32)
    for step in range(1, mp_count):
        target = (mp_here + step) % mp_count
        term = jnp.dot(
            attended,
            lax.dynamic_slice_in_dim(w_out, target * out_cols, out_cols, 1),
            preferred_element_type=jnp.float32,
        ).astype(jnp.bfloat16)
        total = total + passed_along(term, "mp", step).astype(jnp.float32)
    return total.astype(jnp.bfloat16)


def solution(mesh):
    return jax.shard_map(
        on_device,
        mesh=mesh,
        in_specs=(P("seq", "mp"), P(None, None, "mp"), P(), P(), P("mp", None), P(), P()),
        out_specs=P("seq", "mp"),
        check_vma=False,
    )
```

```python
import jax
import jax.numpy as jnp
from jax import lax
from jax.sharding import PartitionSpec as P

HD = 128
TILE = 384
REACH = 4
NB = 6


def passed_along(value, axis, steps):
    count = lax.axis_size(axis)
    pairs = [(source, (source + steps) % count) for source in range(count)]
    return lax.ppermute(value, axis, pairs)


def head_norm(projected, gain_vec):
    per_head = projected.reshape(projected.shape[0], -1, HD)
    factor = lax.rsqrt(jnp.mean(per_head * per_head, axis=-1, keepdims=True) + 1e-06)
    return (per_head * factor * gain_vec).astype(jnp.bfloat16)


def on_device(tokens, w_qkv, q_gain, k_gain, w_out, neighbours, counts):
    tok_rows = tokens.shape[0]
    columns = w_qkv.shape[2]
    heads_here = columns // HD
    tiles_here = tok_rows // TILE
    total_tiles = neighbours.shape[0]
    flat_w = w_qkv.reshape(w_qkv.shape[0], 3 * columns)
    feats = tokens.shape[1]
    mp_count = lax.axis_size("mp")
    mp_here = lax.axis_index("mp")
    projected = jnp.dot(
        tokens,
        lax.dynamic_slice_in_dim(flat_w, mp_here * feats, feats, 0),
        preferred_element_type=jnp.float32,
    )
    for step in range(1, mp_count):
        source = (mp_here - step) % mp_count
        projected = projected + jnp.dot(
            passed_along(tokens, "mp", step),
            lax.dynamic_slice_in_dim(flat_w, source * feats, feats, 0),
            preferred_element_type=jnp.float32,
        )
    queries = head_norm(projected[:, :columns], q_gain)
    key_part = head_norm(projected[:, columns : 2 * columns], k_gain).reshape(tok_rows, columns)
    value_part = projected[:, 2 * columns :].astype(jnp.bfloat16)
    paired = jnp.stack([key_part, value_part])
    position = lax.axis_index("seq")
    seq_count = lax.axis_size("seq")
    core = position % 2
    partner = [(source, source ^ 1) for source in range(seq_count)]
    from_m4 = passed_along(paired, "seq", 4)
    from_m2 = passed_along(paired, "seq", 2)
    from_p2 = passed_along(paired, "seq", -2)
    from_p4 = passed_along(paired, "seq", -4)
    fwd_own = lax.ppermute(paired, "seq", partner)
    fwd_a = lax.ppermute(from_m2, "seq", partner)
    fwd_b = lax.ppermute(from_p2, "seq", partner)
    fwd_c = lax.ppermute(jnp.where(core == 0, from_p4, from_m4), "seq", partner)
    window = jnp.concatenate(
        [paired, from_m4, from_m2, from_p2, from_p4, fwd_own, fwd_a, fwd_b, fwd_c], axis=1
    )
    odd = core == 1
    slot_offsets = jnp.stack(
        [
            jnp.int32(0),
            jnp.int32(-4),
            jnp.int32(-2),
            jnp.int32(2),
            jnp.int32(4),
            jnp.where(odd, -1, 1).astype(jnp.int32),
            jnp.where(odd, -3, -1).astype(jnp.int32),
            jnp.where(odd, 1, 3).astype(jnp.int32),
            jnp.where(odd, 3, -3).astype(jnp.int32),
        ]
    )
    window_tiles = 9
    slot_tile = jnp.mod(position + slot_offsets, total_tiles)
    listed = lax.dynamic_slice_in_dim(neighbours, position, 1, 0)
    used_counts = lax.dynamic_slice_in_dim(counts, position, 1, 0)
    slot_used = jnp.arange(NB, dtype=jnp.int32)[None, :] < used_counts[:, None]
    query_blocks = queries.reshape(tiles_here, TILE, heads_here, HD)
    factor = HD ** (-0.5)
    hits = (listed[:, :, None] == slot_tile[None, None, :]) & slot_used[:, :, None]
    tile_mask = jnp.any(hits, axis=1)
    key_mask = jnp.repeat(tile_mask, TILE, axis=1)
    near_keys = window[0].reshape(window_tiles * TILE, heads_here, HD)
    near_values = window[1].reshape(window_tiles * TILE, heads_here, HD)
    scores = (
        jnp.einsum("tqhd,khd->thqk", query_blocks, near_keys, preferred_element_type=jnp.float32)
        * factor
    )
    scores = jnp.where(key_mask[:, None, None, :], scores, -jnp.inf)
    highest = jnp.max(scores, axis=-1, keepdims=True)
    expo = jnp.exp(scores - highest)
    probs = (expo / jnp.sum(expo, axis=-1, keepdims=True)).astype(jnp.bfloat16)
    attended = jnp.einsum("thqk,khd->tqhd", probs, near_values, preferred_element_type=jnp.float32)
    attended = attended.astype(jnp.bfloat16).reshape(tok_rows, columns)
    out_cols = w_out.shape[1] // mp_count
    total = jnp.dot(
        attended,
        lax.dynamic_slice_in_dim(w_out, mp_here * out_cols, out_cols, 1),
        preferred_element_type=jnp.float32,
    ).astype(jnp.bfloat16).astype(jnp.float32)
    for step in range(1, mp_count):
        target = (mp_here + step) % mp_count
        term = jnp.dot(
            attended,
            lax.dynamic_slice_in_dim(w_out, target * out_cols, out_cols, 1),
            preferred_element_type=jnp.float32,
        ).astype(jnp.bfloat16)
        total = total + passed_along(term, "mp", step).astype(jnp.float32)
    return total.astype(jnp.bfloat16)


def solution(mesh):
    return jax.shard_map(
        on_device,
        mesh=mesh,
        in_specs=(P("seq", "mp"), P(None, None, "mp"), P(), P(), P("mp", None), P(), P()),
        out_specs=P("seq", "mp"),
        check_vma=False,
    )
```

```python
import jax
import jax.numpy as jnp
from jax import lax
from jax.sharding import PartitionSpec as P

HD = 128
TILE = 384
REACH = 4
NB = 6


def passed_along(value, axis, steps):
    count = lax.axis_size(axis)
    pairs = [(source, (source + steps) % count) for source in range(count)]
    return lax.ppermute(value, axis, pairs)


def head_norm(projected, gain_vec):
    per_head = projected.reshape(projected.shape[0], -1, HD)
    factor = lax.rsqrt(jnp.mean(per_head * per_head, axis=-1, keepdims=True) + 1e-06)
    return (per_head * factor * gain_vec).astype(jnp.bfloat16)


def on_device(tokens, w_qkv, q_gain, k_gain, w_out, neighbours, counts):
    tok_rows = tokens.shape[0]
    columns = w_qkv.shape[2]
    heads_here = columns // HD
    tiles_here = tok_rows // TILE
    total_tiles = neighbours.shape[0]
    feats = tokens.shape[1]
    mp_count = lax.axis_size("mp")
    mp_here = lax.axis_index("mp")

    def rows_of(block):
        return lax.dynamic_slice_in_dim(w_qkv, block * feats, feats, 0)

    projected = jnp.einsum(
        "tf,fjc->jtc", tokens, rows_of(mp_here), preferred_element_type=jnp.float32
    )
    for step in range(1, mp_count):
        source = (mp_here - step) % mp_count
        projected = projected + jnp.einsum(
            "tf,fjc->jtc",
            passed_along(tokens, "mp", step),
            rows_of(source),
            preferred_element_type=jnp.float32,
        )
    queries = head_norm(projected[0], q_gain)
    key_part = head_norm(projected[1], k_gain).reshape(tok_rows, columns)
    value_part = projected[2].astype(jnp.bfloat16)
    paired = jnp.stack([key_part, value_part])
    position = lax.axis_index("seq")
    seq_count = lax.axis_size("seq")
    core = position % 2
    partner = [(source, source ^ 1) for source in range(seq_count)]
    from_m4 = passed_along(paired, "seq", 4)
    from_m2 = passed_along(paired, "seq", 2)
    from_p2 = passed_along(paired, "seq", -2)
    from_p4 = passed_along(paired, "seq", -4)
    fwd_own = lax.ppermute(paired, "seq", partner)
    fwd_a = lax.ppermute(from_m2, "seq", partner)
    fwd_b = lax.ppermute(from_p2, "seq", partner)
    fwd_c = lax.ppermute(jnp.where(core == 0, from_p4, from_m4), "seq", partner)
    window = jnp.concatenate(
        [paired, from_m4, from_m2, from_p2, from_p4, fwd_own, fwd_a, fwd_b, fwd_c], axis=1
    )
    odd = core == 1
    slot_offsets = jnp.stack(
        [
            jnp.int32(0),
            jnp.int32(-4),
            jnp.int32(-2),
            jnp.int32(2),
            jnp.int32(4),
            jnp.where(odd, -1, 1).astype(jnp.int32),
            jnp.where(odd, -3, -1).astype(jnp.int32),
            jnp.where(odd, 1, 3).astype(jnp.int32),
            jnp.where(odd, 3, -3).astype(jnp.int32),
        ]
    )
    window_tiles = 9
    slot_tile = jnp.mod(position + slot_offsets, total_tiles)
    listed = lax.dynamic_slice_in_dim(neighbours, position, 1, 0)
    used_counts = lax.dynamic_slice_in_dim(counts, position, 1, 0)
    slot_used = jnp.arange(NB, dtype=jnp.int32)[None, :] < used_counts[:, None]
    query_blocks = queries.reshape(tiles_here, TILE, heads_here, HD)
    factor = HD ** (-0.5)
    hits = (listed[:, :, None] == slot_tile[None, None, :]) & slot_used[:, :, None]
    tile_mask = jnp.any(hits, axis=1)
    key_mask = jnp.repeat(tile_mask, TILE, axis=1)
    near_keys = window[0].reshape(window_tiles * TILE, heads_here, HD)
    near_values = window[1].reshape(window_tiles * TILE, heads_here, HD)
    scores = (
        jnp.einsum("tqhd,khd->thqk", query_blocks, near_keys, preferred_element_type=jnp.float32)
        * factor
    )
    scores = jnp.where(key_mask[:, None, None, :], scores, -jnp.inf)
    highest = jnp.max(scores, axis=-1, keepdims=True)
    expo = jnp.exp(scores - highest)
    probs = (expo / jnp.sum(expo, axis=-1, keepdims=True)).astype(jnp.bfloat16)
    attended = jnp.einsum("thqk,khd->tqhd", probs, near_values, preferred_element_type=jnp.float32)
    attended = attended.astype(jnp.bfloat16).reshape(tok_rows, columns)
    out_cols = w_out.shape[1] // mp_count
    total = jnp.dot(
        attended,
        lax.dynamic_slice_in_dim(w_out, mp_here * out_cols, out_cols, 1),
        preferred_element_type=jnp.float32,
    ).astype(jnp.bfloat16).astype(jnp.float32)
    for step in range(1, mp_count):
        target = (mp_here + step) % mp_count
        term = jnp.dot(
            attended,
            lax.dynamic_slice_in_dim(w_out, target * out_cols, out_cols, 1),
            preferred_element_type=jnp.float32,
        ).astype(jnp.bfloat16)
        total = total + passed_along(term, "mp", step).astype(jnp.float32)
    return total.astype(jnp.bfloat16)


def solution(mesh):
    return jax.shard_map(
        on_device,
        mesh=mesh,
        in_specs=(P("seq", "mp"), P(None, None, "mp"), P(), P(), P("mp", None), P(), P()),
        out_specs=P("seq", "mp"),
        check_vma=False,
    )
```

```python
import jax
import jax.numpy as jnp
from jax import lax
from jax.experimental import pallas as pl
from jax.experimental.pallas import tpu as pltpu
from jax.sharding import PartitionSpec as P

HD = 128
TILE = 384
REACH = 4
NB = 6


def passed_along(value, axis, steps):
    count = lax.axis_size(axis)
    pairs = [(source, (source + steps) % count) for source in range(count)]
    return lax.ppermute(value, axis, pairs)


def head_norm(projected, gain_vec):
    per_head = projected.reshape(projected.shape[0], -1, HD)
    factor = lax.rsqrt(jnp.mean(per_head * per_head, axis=-1, keepdims=True) + 1e-06)
    return (per_head * factor * gain_vec).astype(jnp.bfloat16)


def attend_kernel(mask_ref, q_ref, *rest):
    slots = len(rest) - 5
    kv_refs = rest[:slots]
    out_ref = rest[slots]
    s_ref, m_ref, l_ref, acc_ref = rest[slots + 1 :]
    factor = HD ** (-0.5)
    q = q_ref[...]
    m_ref[...] = jnp.full(m_ref.shape, -jnp.inf, jnp.float32)
    l_ref[...] = jnp.zeros(l_ref.shape, jnp.float32)
    acc_ref[...] = jnp.zeros(acc_ref.shape, jnp.float32)
    for i in range(slots):
        @pl.when(mask_ref[i] > 0)
        def _():
            s = lax.dot_general(
                q, kv_refs[i][0], (((1,), (1,)), ((), ())), preferred_element_type=jnp.float32
            ) * factor
            s_ref[i] = s
            m_ref[...] = jnp.maximum(m_ref[...], jnp.max(s, axis=-1, keepdims=True))
    for i in range(slots):
        @pl.when(mask_ref[i] > 0)
        def _():
            e = jnp.exp(s_ref[i] - m_ref[...])
            s_ref[i] = e
            l_ref[...] = l_ref[...] + jnp.sum(e, axis=-1, keepdims=True)
    for i in range(slots):
        @pl.when(mask_ref[i] > 0)
        def _():
            p = (s_ref[i] / l_ref[...]).astype(jnp.bfloat16)
            acc_ref[...] = acc_ref[...] + jnp.dot(
                p, kv_refs[i][1], preferred_element_type=jnp.float32
            )
    out_ref[...] = acc_ref[...].astype(jnp.bfloat16)


def attend(slot_mask, queries, kv_tiles):
    rows, columns = queries.shape
    heads = columns // HD
    keys = kv_tiles[0].shape[1]
    slots = len(kv_tiles)
    q_spec = pl.BlockSpec((rows, HD), lambda h, mask: (0, h))
    kv_spec = pl.BlockSpec((2, keys, HD), lambda h, mask: (0, 0, h))
    return pl.pallas_call(
        attend_kernel,
        grid_spec=pltpu.PrefetchScalarGridSpec(
            num_scalar_prefetch=1,
            grid=(heads,),
            in_specs=[q_spec] + [kv_spec] * slots,
            out_specs=pl.BlockSpec((rows, HD), lambda h, mask: (0, h)),
            scratch_shapes=[
                pltpu.VMEM((slots, rows, keys), jnp.float32),
                pltpu.VMEM((rows, 1), jnp.float32),
                pltpu.VMEM((rows, 1), jnp.float32),
                pltpu.VMEM((rows, HD), jnp.float32),
            ],
        ),
        out_shape=jax.ShapeDtypeStruct((rows, columns), jnp.bfloat16),
    )(slot_mask, queries, *kv_tiles)


def on_device(tokens, w_qkv, q_gain, k_gain, w_out, neighbours, counts):
    tok_rows = tokens.shape[0]
    columns = w_qkv.shape[2]
    heads_here = columns // HD
    tiles_here = tok_rows // TILE
    total_tiles = neighbours.shape[0]
    feats = tokens.shape[1]
    mp_count = lax.axis_size("mp")
    mp_here = lax.axis_index("mp")

    def rows_of(block):
        return lax.dynamic_slice_in_dim(w_qkv, block * feats, feats, 0)

    projected = jnp.einsum(
        "tf,fjc->jtc", tokens, rows_of(mp_here), preferred_element_type=jnp.float32
    )
    for step in range(1, mp_count):
        source = (mp_here - step) % mp_count
        projected = projected + jnp.einsum(
            "tf,fjc->jtc",
            passed_along(tokens, "mp", step),
            rows_of(source),
            preferred_element_type=jnp.float32,
        )
    queries = head_norm(projected[0], q_gain)
    key_part = head_norm(projected[1], k_gain).reshape(tok_rows, columns)
    value_part = projected[2].astype(jnp.bfloat16)
    paired = jnp.stack([key_part, value_part])
    position = lax.axis_index("seq")
    seq_count = lax.axis_size("seq")
    core = position % 2
    partner = [(source, source ^ 1) for source in range(seq_count)]
    from_m4 = passed_along(paired, "seq", 4)
    from_m2 = passed_along(paired, "seq", 2)
    from_p2 = passed_along(paired, "seq", -2)
    from_p4 = passed_along(paired, "seq", -4)
    fwd_own = lax.ppermute(paired, "seq", partner)
    fwd_a = lax.ppermute(from_m2, "seq", partner)
    fwd_b = lax.ppermute(from_p2, "seq", partner)
    fwd_c = lax.ppermute(jnp.where(core == 0, from_p4, from_m4), "seq", partner)
    kv_tiles = [paired, from_m4, from_m2, from_p2, from_p4, fwd_own, fwd_a, fwd_b, fwd_c]
    odd = core == 1
    slot_offsets = jnp.stack(
        [
            jnp.int32(0),
            jnp.int32(-4),
            jnp.int32(-2),
            jnp.int32(2),
            jnp.int32(4),
            jnp.where(odd, -1, 1).astype(jnp.int32),
            jnp.where(odd, -3, -1).astype(jnp.int32),
            jnp.where(odd, 1, 3).astype(jnp.int32),
            jnp.where(odd, 3, -3).astype(jnp.int32),
        ]
    )
    slot_tile = jnp.mod(position + slot_offsets, total_tiles)
    listed = lax.dynamic_slice_in_dim(neighbours, position, 1, 0)
    used_counts = lax.dynamic_slice_in_dim(counts, position, 1, 0)
    slot_used = jnp.arange(NB, dtype=jnp.int32)[None, :] < used_counts[:, None]
    hits = (listed[:, :, None] == slot_tile[None, None, :]) & slot_used[:, :, None]
    tile_mask = jnp.any(hits, axis=1)[0].astype(jnp.int32)
    attended = attend(tile_mask, queries.reshape(tok_rows, columns), kv_tiles)
    out_cols = w_out.shape[1] // mp_count
    total = jnp.dot(
        attended,
        lax.dynamic_slice_in_dim(w_out, mp_here * out_cols, out_cols, 1),
        preferred_element_type=jnp.float32,
    ).astype(jnp.bfloat16).astype(jnp.float32)
    for step in range(1, mp_count):
        target = (mp_here + step) % mp_count
        term = jnp.dot(
            attended,
            lax.dynamic_slice_in_dim(w_out, target * out_cols, out_cols, 1),
            preferred_element_type=jnp.float32,
        ).astype(jnp.bfloat16)
        total = total + passed_along(term, "mp", step).astype(jnp.float32)
    return total.astype(jnp.bfloat16)


def solution(mesh):
    return jax.shard_map(
        on_device,
        mesh=mesh,
        in_specs=(P("seq", "mp"), P(None, None, "mp"), P(), P(), P("mp", None), P(), P()),
        out_specs=P("seq", "mp"),
        check_vma=False,
    )
```

```python
import jax
import jax.numpy as jnp
from jax import lax
from jax.experimental import pallas as pl
from jax.experimental.pallas import tpu as pltpu
from jax.sharding import PartitionSpec as P

HD = 128
TILE = 384
REACH = 4
NB = 6


def passed_along(value, axis, steps):
    count = lax.axis_size(axis)
    pairs = [(source, (source + steps) % count) for source in range(count)]
    return lax.ppermute(value, axis, pairs)


def head_norm(projected, gain_vec):
    per_head = projected.reshape(projected.shape[0], -1, HD)
    factor = lax.rsqrt(jnp.mean(per_head * per_head, axis=-1, keepdims=True) + 1e-06)
    return (per_head * factor * gain_vec).astype(jnp.bfloat16)


def attend_kernel(mask_ref, q_ref, gain_ref, *rest):
    slots = len(rest) - 4
    kv_refs = rest[:slots]
    out_ref = rest[slots]
    m_ref, l_ref, acc_ref = rest[slots + 1 :]
    factor = HD ** (-0.5)
    q_raw = q_ref[...]
    norm = lax.rsqrt(jnp.mean(q_raw * q_raw, axis=-1, keepdims=True) + 1e-06)
    q = (q_raw * norm * gain_ref[...]).astype(jnp.bfloat16)
    m_ref[...] = jnp.full(m_ref.shape, -jnp.inf, jnp.float32)
    l_ref[...] = jnp.zeros(l_ref.shape, jnp.float32)
    acc_ref[...] = jnp.zeros(acc_ref.shape, jnp.float32)
    for i in range(slots):
        @pl.when(mask_ref[i] > 0)
        def _():
            s = lax.dot_general(
                q, kv_refs[i][0], (((1,), (1,)), ((), ())), preferred_element_type=jnp.float32
            )
            m_prev = m_ref[...]
            m_new = jnp.maximum(m_prev, jnp.max(s, axis=-1, keepdims=True))
            alpha = jnp.exp((m_prev - m_new) * factor)
            p = jnp.exp((s - m_new) * factor)
            l_ref[...] = alpha * l_ref[...] + jnp.sum(p, axis=-1, keepdims=True)
            acc_ref[...] = alpha * acc_ref[...] + jnp.dot(
                p.astype(jnp.bfloat16), kv_refs[i][1], preferred_element_type=jnp.float32
            )
            m_ref[...] = m_new
    out_ref[...] = (acc_ref[...] / l_ref[...]).astype(jnp.bfloat16)


def attend(slot_mask, q_raw, q_gain, kv_tiles):
    rows, columns = q_raw.shape
    heads = columns // HD
    keys = kv_tiles[0].shape[1]
    slots = len(kv_tiles)
    kv_spec = pl.BlockSpec((2, keys, HD), lambda h, mask: (0, 0, h))
    return pl.pallas_call(
        attend_kernel,
        grid_spec=pltpu.PrefetchScalarGridSpec(
            num_scalar_prefetch=1,
            grid=(heads,),
            in_specs=[
                pl.BlockSpec((rows, HD), lambda h, mask: (0, h)),
                pl.BlockSpec((1, HD), lambda h, mask: (0, 0)),
            ]
            + [kv_spec] * slots,
            out_specs=pl.BlockSpec((rows, HD), lambda h, mask: (0, h)),
            scratch_shapes=[
                pltpu.VMEM((rows, 1), jnp.float32),
                pltpu.VMEM((rows, 1), jnp.float32),
                pltpu.VMEM((rows, HD), jnp.float32),
            ],
        ),
        out_shape=jax.ShapeDtypeStruct((rows, columns), jnp.bfloat16),
    )(slot_mask, q_raw, q_gain.reshape(1, HD), *kv_tiles)


def on_device(tokens, w_qkv, q_gain, k_gain, w_out, neighbours, counts):
    tok_rows = tokens.shape[0]
    columns = w_qkv.shape[2]
    heads_here = columns // HD
    tiles_here = tok_rows // TILE
    total_tiles = neighbours.shape[0]
    feats = tokens.shape[1]
    mp_count = lax.axis_size("mp")
    mp_here = lax.axis_index("mp")

    def rows_of(block):
        return lax.dynamic_slice_in_dim(w_qkv, block * feats, feats, 0)

    projected = jnp.einsum(
        "tf,fjc->jtc", tokens, rows_of(mp_here), preferred_element_type=jnp.float32
    )
    for step in range(1, mp_count):
        source = (mp_here - step) % mp_count
        projected = projected + jnp.einsum(
            "tf,fjc->jtc",
            passed_along(tokens, "mp", step),
            rows_of(source),
            preferred_element_type=jnp.float32,
        )
    key_part = head_norm(projected[1], k_gain).reshape(tok_rows, columns)
    value_part = projected[2].astype(jnp.bfloat16)
    paired = jnp.stack([key_part, value_part])
    position = lax.axis_index("seq")
    seq_count = lax.axis_size("seq")
    core = position % 2
    partner = [(source, source ^ 1) for source in range(seq_count)]
    from_m4 = passed_along(paired, "seq", 4)
    from_m2 = passed_along(paired, "seq", 2)
    from_p2 = passed_along(paired, "seq", -2)
    from_p4 = passed_along(paired, "seq", -4)
    fwd_own = lax.ppermute(paired, "seq", partner)
    fwd_a = lax.ppermute(from_m2, "seq", partner)
    fwd_b = lax.ppermute(from_p2, "seq", partner)
    fwd_c = lax.ppermute(jnp.where(core == 0, from_p4, from_m4), "seq", partner)
    kv_tiles = [paired, from_m4, from_m2, from_p2, from_p4, fwd_own, fwd_a, fwd_b, fwd_c]
    odd = core == 1
    slot_offsets = jnp.stack(
        [
            jnp.int32(0),
            jnp.int32(-4),
            jnp.int32(-2),
            jnp.int32(2),
            jnp.int32(4),
            jnp.where(odd, -1, 1).astype(jnp.int32),
            jnp.where(odd, -3, -1).astype(jnp.int32),
            jnp.where(odd, 1, 3).astype(jnp.int32),
            jnp.where(odd, 3, -3).astype(jnp.int32),
        ]
    )
    slot_tile = jnp.mod(position + slot_offsets, total_tiles)
    listed = lax.dynamic_slice_in_dim(neighbours, position, 1, 0)
    used_counts = lax.dynamic_slice_in_dim(counts, position, 1, 0)
    slot_used = jnp.arange(NB, dtype=jnp.int32)[None, :] < used_counts[:, None]
    hits = (listed[:, :, None] == slot_tile[None, None, :]) & slot_used[:, :, None]
    tile_mask = jnp.any(hits, axis=1)[0].astype(jnp.int32)
    attended = attend(tile_mask, projected[0], q_gain, kv_tiles)
    out_cols = w_out.shape[1] // mp_count
    total = jnp.dot(
        attended,
        lax.dynamic_slice_in_dim(w_out, mp_here * out_cols, out_cols, 1),
        preferred_element_type=jnp.float32,
    ).astype(jnp.bfloat16).astype(jnp.float32)
    for step in range(1, mp_count):
        target = (mp_here + step) % mp_count
        term = jnp.dot(
            attended,
            lax.dynamic_slice_in_dim(w_out, target * out_cols, out_cols, 1),
            preferred_element_type=jnp.float32,
        ).astype(jnp.bfloat16)
        total = total + passed_along(term, "mp", step).astype(jnp.float32)
    return total.astype(jnp.bfloat16)


def solution(mesh):
    return jax.shard_map(
        on_device,
        mesh=mesh,
        in_specs=(P("seq", "mp"), P(None, None, "mp"), P(), P(), P("mp", None), P(), P()),
        out_specs=P("seq", "mp"),
        check_vma=False,
    )
```

```python
import jax
import jax.numpy as jnp
from jax import lax
from jax.experimental import pallas as pl
from jax.experimental.pallas import tpu as pltpu
from jax.sharding import PartitionSpec as P

HD = 128
TILE = 384
REACH = 4
NB = 6


def passed_along(value, axis, steps):
    count = lax.axis_size(axis)
    pairs = [(source, (source + steps) % count) for source in range(count)]
    return lax.ppermute(value, axis, pairs)


def head_norm(projected, gain_vec):
    per_head = projected.reshape(projected.shape[0], -1, HD)
    factor = lax.rsqrt(jnp.mean(per_head * per_head, axis=-1, keepdims=True) + 1e-06)
    return (per_head * factor * gain_vec).astype(jnp.bfloat16)


def attend_kernel(mask_ref, q_ref, gain_ref, *rest):
    slots = len(rest) - 4
    kv_refs = rest[:slots]
    out_ref = rest[slots]
    m_ref, l_ref, acc_ref = rest[slots + 1 :]
    factor = HD ** (-0.5)
    q_raw = q_ref[...]
    norm = lax.rsqrt(jnp.mean(q_raw * q_raw, axis=-1, keepdims=True) + 1e-06)
    q = (q_raw * norm * gain_ref[...]).astype(jnp.bfloat16)
    m_ref[...] = jnp.full(m_ref.shape, -jnp.inf, jnp.float32)
    l_ref[...] = jnp.zeros(l_ref.shape, jnp.float32)
    acc_ref[...] = jnp.zeros(acc_ref.shape, jnp.float32)

    def scores_of(i):
        return lax.dot_general(
            q, kv_refs[i][0], (((1,), (1,)), ((), ())), preferred_element_type=jnp.float32
        )

    for i in range(slots):
        @pl.when(mask_ref[i] > 0)
        def _():
            m_ref[...] = jnp.maximum(m_ref[...], scores_of(i))
    highest = jnp.max(m_ref[...], axis=-1, keepdims=True)
    for i in range(slots):
        @pl.when(mask_ref[i] > 0)
        def _():
            p = jnp.exp((scores_of(i) - highest) * factor)
            l_ref[...] = l_ref[...] + p
            acc_ref[...] = acc_ref[...] + jnp.dot(
                p.astype(jnp.bfloat16), kv_refs[i][1], preferred_element_type=jnp.float32
            )
    total = jnp.sum(l_ref[...], axis=-1, keepdims=True)
    out_ref[...] = (acc_ref[...] / total).astype(jnp.bfloat16)


def attend(slot_mask, q_raw, q_gain, kv_tiles):
    rows, columns = q_raw.shape
    heads = columns // HD
    keys = kv_tiles[0].shape[1]
    slots = len(kv_tiles)
    kv_spec = pl.BlockSpec((2, keys, HD), lambda h, mask: (0, 0, h))
    return pl.pallas_call(
        attend_kernel,
        grid_spec=pltpu.PrefetchScalarGridSpec(
            num_scalar_prefetch=1,
            grid=(heads,),
            in_specs=[
                pl.BlockSpec((rows, HD), lambda h, mask: (0, h)),
                pl.BlockSpec((1, HD), lambda h, mask: (0, 0)),
            ]
            + [kv_spec] * slots,
            out_specs=pl.BlockSpec((rows, HD), lambda h, mask: (0, h)),
            scratch_shapes=[
                pltpu.VMEM((rows, keys), jnp.float32),
                pltpu.VMEM((rows, keys), jnp.float32),
                pltpu.VMEM((rows, HD), jnp.float32),
            ],
        ),
        out_shape=jax.ShapeDtypeStruct((rows, columns), jnp.bfloat16),
    )(slot_mask, q_raw, q_gain.reshape(1, HD), *kv_tiles)


def on_device(tokens, w_qkv, q_gain, k_gain, w_out, neighbours, counts):
    tok_rows = tokens.shape[0]
    columns = w_qkv.shape[2]
    heads_here = columns // HD
    tiles_here = tok_rows // TILE
    total_tiles = neighbours.shape[0]
    feats = tokens.shape[1]
    mp_count = lax.axis_size("mp")
    mp_here = lax.axis_index("mp")

    def rows_of(block):
        return lax.dynamic_slice_in_dim(w_qkv, block * feats, feats, 0)

    projected = jnp.einsum(
        "tf,fjc->jtc", tokens, rows_of(mp_here), preferred_element_type=jnp.float32
    )
    for step in range(1, mp_count):
        source = (mp_here - step) % mp_count
        projected = projected + jnp.einsum(
            "tf,fjc->jtc",
            passed_along(tokens, "mp", step),
            rows_of(source),
            preferred_element_type=jnp.float32,
        )
    key_part = head_norm(projected[1], k_gain).reshape(tok_rows, columns)
    value_part = projected[2].astype(jnp.bfloat16)
    paired = jnp.stack([key_part, value_part])
    position = lax.axis_index("seq")
    seq_count = lax.axis_size("seq")
    core = position % 2
    partner = [(source, source ^ 1) for source in range(seq_count)]
    from_m4 = passed_along(paired, "seq", 4)
    from_m2 = passed_along(paired, "seq", 2)
    from_p2 = passed_along(paired, "seq", -2)
    from_p4 = passed_along(paired, "seq", -4)
    fwd_own = lax.ppermute(paired, "seq", partner)
    fwd_a = lax.ppermute(from_m2, "seq", partner)
    fwd_b = lax.ppermute(from_p2, "seq", partner)
    fwd_c = lax.ppermute(jnp.where(core == 0, from_p4, from_m4), "seq", partner)
    kv_tiles = [paired, from_m4, from_m2, from_p2, from_p4, fwd_own, fwd_a, fwd_b, fwd_c]
    odd = core == 1
    slot_offsets = jnp.stack(
        [
            jnp.int32(0),
            jnp.int32(-4),
            jnp.int32(-2),
            jnp.int32(2),
            jnp.int32(4),
            jnp.where(odd, -1, 1).astype(jnp.int32),
            jnp.where(odd, -3, -1).astype(jnp.int32),
            jnp.where(odd, 1, 3).astype(jnp.int32),
            jnp.where(odd, 3, -3).astype(jnp.int32),
        ]
    )
    slot_tile = jnp.mod(position + slot_offsets, total_tiles)
    listed = lax.dynamic_slice_in_dim(neighbours, position, 1, 0)
    used_counts = lax.dynamic_slice_in_dim(counts, position, 1, 0)
    slot_used = jnp.arange(NB, dtype=jnp.int32)[None, :] < used_counts[:, None]
    hits = (listed[:, :, None] == slot_tile[None, None, :]) & slot_used[:, :, None]
    tile_mask = jnp.any(hits, axis=1)[0].astype(jnp.int32)
    attended = attend(tile_mask, projected[0], q_gain, kv_tiles)
    out_cols = w_out.shape[1] // mp_count
    total = jnp.dot(
        attended,
        lax.dynamic_slice_in_dim(w_out, mp_here * out_cols, out_cols, 1),
        preferred_element_type=jnp.float32,
    ).astype(jnp.bfloat16).astype(jnp.float32)
    for step in range(1, mp_count):
        target = (mp_here + step) % mp_count
        term = jnp.dot(
            attended,
            lax.dynamic_slice_in_dim(w_out, target * out_cols, out_cols, 1),
            preferred_element_type=jnp.float32,
        ).astype(jnp.bfloat16)
        total = total + passed_along(term, "mp", step).astype(jnp.float32)
    return total.astype(jnp.bfloat16)


def solution(mesh):
    return jax.shard_map(
        on_device,
        mesh=mesh,
        in_specs=(P("seq", "mp"), P(None, None, "mp"), P(), P(), P("mp", None), P(), P()),
        out_specs=P("seq", "mp"),
        check_vma=False,
    )
```

```python
import jax
import jax.numpy as jnp
from jax import lax
from jax.experimental import pallas as pl
from jax.experimental.pallas import tpu as pltpu
from jax.sharding import PartitionSpec as P

HD = 128
TILE = 384
REACH = 4
NB = 6


def passed_along(value, axis, steps):
    count = lax.axis_size(axis)
    pairs = [(source, (source + steps) % count) for source in range(count)]
    return lax.ppermute(value, axis, pairs)


def head_norm(projected, gain_vec):
    per_head = projected.reshape(projected.shape[0], -1, HD)
    factor = lax.rsqrt(jnp.mean(per_head * per_head, axis=-1, keepdims=True) + 1e-06)
    return (per_head * factor * gain_vec).astype(jnp.bfloat16)


def attend_kernel(mask_ref, q_ref, gain_ref, *rest):
    slots = len(rest) - 4
    kv_refs = rest[:slots]
    out_ref = rest[slots]
    m_ref, l_ref, acc_ref = rest[slots + 1 :]
    factor = HD ** (-0.5)
    q_raw = q_ref[...]
    norm = lax.rsqrt(jnp.mean(q_raw * q_raw, axis=-1, keepdims=True) + 1e-06)
    q = (q_raw * norm * gain_ref[...]).astype(jnp.bfloat16)
    m_ref[...] = jnp.full(m_ref.shape, -jnp.inf, jnp.float32)
    l_ref[...] = jnp.zeros(l_ref.shape, jnp.float32)
    acc_ref[...] = jnp.zeros(acc_ref.shape, jnp.float32)

    def scores_of(i):
        return lax.dot_general(
            q, kv_refs[i][0], (((1,), (1,)), ((), ())), preferred_element_type=jnp.float32
        )

    for i in range(slots):
        @pl.when(mask_ref[i] > 0)
        def _():
            m_ref[...] = jnp.maximum(m_ref[...], scores_of(i))
    highest = jnp.max(m_ref[...], axis=-1, keepdims=True)
    for i in range(slots):
        @pl.when(mask_ref[i] > 0)
        def _():
            p = jnp.exp((scores_of(i) - highest) * factor)
            l_ref[...] = l_ref[...] + p
            acc_ref[...] = acc_ref[...] + jnp.dot(
                p.astype(jnp.bfloat16), kv_refs[i][1], preferred_element_type=jnp.float32
            )
    total = jnp.sum(l_ref[...], axis=-1, keepdims=True)
    out_ref[...] = (acc_ref[...] / total).astype(jnp.bfloat16)


def attend(slot_mask, q_raw, q_gain, kv_tiles):
    heads, rows, _ = q_raw.shape
    columns = heads * HD
    keys = kv_tiles[0].shape[2]
    slots = len(kv_tiles)
    kv_spec = pl.BlockSpec((2, None, keys, HD), lambda h, mask: (0, h, 0, 0))
    return pl.pallas_call(
        attend_kernel,
        grid_spec=pltpu.PrefetchScalarGridSpec(
            num_scalar_prefetch=1,
            grid=(heads,),
            in_specs=[
                pl.BlockSpec((None, rows, HD), lambda h, mask: (h, 0, 0)),
                pl.BlockSpec((1, HD), lambda h, mask: (0, 0)),
            ]
            + [kv_spec] * slots,
            out_specs=pl.BlockSpec((rows, HD), lambda h, mask: (0, h)),
            scratch_shapes=[
                pltpu.VMEM((rows, keys), jnp.float32),
                pltpu.VMEM((rows, keys), jnp.float32),
                pltpu.VMEM((rows, HD), jnp.float32),
            ],
        ),
        out_shape=jax.ShapeDtypeStruct((rows, columns), jnp.bfloat16),
    )(slot_mask, q_raw, q_gain.reshape(1, HD), *kv_tiles)


def on_device(tokens, w_qkv, q_gain, k_gain, w_out, neighbours, counts):
    tok_rows = tokens.shape[0]
    columns = w_qkv.shape[2]
    heads_here = columns // HD
    tiles_here = tok_rows // TILE
    total_tiles = neighbours.shape[0]
    feats = tokens.shape[1]
    mp_count = lax.axis_size("mp")
    mp_here = lax.axis_index("mp")

    def rows_of(block):
        return lax.dynamic_slice_in_dim(w_qkv, block * feats, feats, 0)

    projected = jnp.einsum(
        "tf,fjc->jtc", tokens, rows_of(mp_here), preferred_element_type=jnp.float32
    )
    for step in range(1, mp_count):
        source = (mp_here - step) % mp_count
        projected = projected + jnp.einsum(
            "tf,fjc->jtc",
            passed_along(tokens, "mp", step),
            rows_of(source),
            preferred_element_type=jnp.float32,
        )
    key_part = head_norm(projected[1], k_gain).transpose(1, 0, 2)
    value_part = projected[2].astype(jnp.bfloat16).reshape(tok_rows, heads_here, HD).transpose(1, 0, 2)
    paired = jnp.stack([key_part, value_part])
    position = lax.axis_index("seq")
    seq_count = lax.axis_size("seq")
    core = position % 2
    partner = [(source, source ^ 1) for source in range(seq_count)]
    from_m4 = passed_along(paired, "seq", 4)
    from_m2 = passed_along(paired, "seq", 2)
    from_p2 = passed_along(paired, "seq", -2)
    from_p4 = passed_along(paired, "seq", -4)
    fwd_own = lax.ppermute(paired, "seq", partner)
    fwd_a = lax.ppermute(from_m2, "seq", partner)
    fwd_b = lax.ppermute(from_p2, "seq", partner)
    fwd_c = lax.ppermute(jnp.where(core == 0, from_p4, from_m4), "seq", partner)
    kv_tiles = [paired, from_m4, from_m2, from_p2, from_p4, fwd_own, fwd_a, fwd_b, fwd_c]
    odd = core == 1
    slot_offsets = jnp.stack(
        [
            jnp.int32(0),
            jnp.int32(-4),
            jnp.int32(-2),
            jnp.int32(2),
            jnp.int32(4),
            jnp.where(odd, -1, 1).astype(jnp.int32),
            jnp.where(odd, -3, -1).astype(jnp.int32),
            jnp.where(odd, 1, 3).astype(jnp.int32),
            jnp.where(odd, 3, -3).astype(jnp.int32),
        ]
    )
    slot_tile = jnp.mod(position + slot_offsets, total_tiles)
    listed = lax.dynamic_slice_in_dim(neighbours, position, 1, 0)
    used_counts = lax.dynamic_slice_in_dim(counts, position, 1, 0)
    slot_used = jnp.arange(NB, dtype=jnp.int32)[None, :] < used_counts[:, None]
    hits = (listed[:, :, None] == slot_tile[None, None, :]) & slot_used[:, :, None]
    tile_mask = jnp.any(hits, axis=1)[0].astype(jnp.int32)
    q_raw = projected[0].reshape(tok_rows, heads_here, HD).transpose(1, 0, 2)
    attended = attend(tile_mask, q_raw, q_gain, kv_tiles)
    out_cols = w_out.shape[1] // mp_count
    total = jnp.dot(
        attended,
        lax.dynamic_slice_in_dim(w_out, mp_here * out_cols, out_cols, 1),
        preferred_element_type=jnp.float32,
    ).astype(jnp.bfloat16).astype(jnp.float32)
    for step in range(1, mp_count):
        target = (mp_here + step) % mp_count
        term = jnp.dot(
            attended,
            lax.dynamic_slice_in_dim(w_out, target * out_cols, out_cols, 1),
            preferred_element_type=jnp.float32,
        ).astype(jnp.bfloat16)
        total = total + passed_along(term, "mp", step).astype(jnp.float32)
    return total.astype(jnp.bfloat16)


def solution(mesh):
    return jax.shard_map(
        on_device,
        mesh=mesh,
        in_specs=(P("seq", "mp"), P(None, None, "mp"), P(), P(), P("mp", None), P(), P()),
        out_specs=P("seq", "mp"),
        check_vma=False,
    )
```

```python
import jax
import jax.numpy as jnp
from jax import lax
from jax.experimental import pallas as pl
from jax.experimental.pallas import tpu as pltpu
from jax.sharding import PartitionSpec as P

HD = 128
TILE = 384
REACH = 4
NB = 6


def passed_along(value, axis, steps):
    count = lax.axis_size(axis)
    pairs = [(source, (source + steps) % count) for source in range(count)]
    return lax.ppermute(value, axis, pairs)


def head_norm(projected, gain_vec):
    per_head = projected.reshape(projected.shape[0], -1, HD)
    factor = lax.rsqrt(jnp.mean(per_head * per_head, axis=-1, keepdims=True) + 1e-06)
    return (per_head * factor * gain_vec).astype(jnp.bfloat16)


def attend_kernel(mask_ref, q_ref, gain_ref, *rest):
    slots = len(rest) - 4
    kv_refs = rest[:slots]
    out_ref = rest[slots]
    m_ref, l_ref, acc_ref = rest[slots + 1 :]
    factor = HD ** (-0.5)
    q_raw = q_ref[...]
    norm = lax.rsqrt(jnp.mean(q_raw * q_raw, axis=-1, keepdims=True) + 1e-06)
    q = (q_raw * norm * gain_ref[...]).astype(jnp.bfloat16)
    m_ref[...] = jnp.full(m_ref.shape, -jnp.inf, jnp.float32)
    l_ref[...] = jnp.zeros(l_ref.shape, jnp.float32)
    acc_ref[...] = jnp.zeros(acc_ref.shape, jnp.float32)

    def scores_of(i):
        return lax.dot_general(
            q, kv_refs[i][0], (((1,), (1,)), ((), ())), preferred_element_type=jnp.float32
        )

    for i in range(slots):
        @pl.when(mask_ref[i] > 0)
        def _():
            m_ref[...] = jnp.maximum(m_ref[...], scores_of(i))
    highest = jnp.max(m_ref[...], axis=-1, keepdims=True)
    for i in range(slots):
        @pl.when(mask_ref[i] > 0)
        def _():
            p = jnp.exp((scores_of(i) - highest) * factor)
            l_ref[...] = l_ref[...] + p
            acc_ref[...] = acc_ref[...] + jnp.dot(
                p.astype(jnp.bfloat16), kv_refs[i][1], preferred_element_type=jnp.float32
            )
    total = jnp.sum(l_ref[...], axis=-1, keepdims=True)
    out_ref[...] = (acc_ref[...] / total).astype(jnp.bfloat16)


def attend(slot_mask, q_raw, q_gain, kv_tiles):
    heads, rows, _ = q_raw.shape
    columns = heads * HD
    keys = kv_tiles[0].shape[2]
    slots = len(kv_tiles)
    kv_spec = pl.BlockSpec((2, None, keys, HD), lambda h, mask: (0, h, 0, 0))
    return pl.pallas_call(
        attend_kernel,
        grid_spec=pltpu.PrefetchScalarGridSpec(
            num_scalar_prefetch=1,
            grid=(heads,),
            in_specs=[
                pl.BlockSpec((None, rows, HD), lambda h, mask: (h, 0, 0)),
                pl.BlockSpec((1, HD), lambda h, mask: (0, 0)),
            ]
            + [kv_spec] * slots,
            out_specs=pl.BlockSpec((rows, HD), lambda h, mask: (0, h)),
            scratch_shapes=[
                pltpu.VMEM((rows, keys), jnp.float32),
                pltpu.VMEM((rows, keys), jnp.float32),
                pltpu.VMEM((rows, HD), jnp.float32),
            ],
        ),
        out_shape=jax.ShapeDtypeStruct((rows, columns), jnp.bfloat16),
    )(slot_mask, q_raw, q_gain.reshape(1, HD), *kv_tiles)


def on_device(tokens, w_qkv, q_gain, k_gain, w_out, neighbours, counts):
    tok_rows = tokens.shape[0]
    columns = w_qkv.shape[2]
    heads_here = columns // HD
    tiles_here = tok_rows // TILE
    total_tiles = neighbours.shape[0]
    feats = tokens.shape[1]
    mp_count = lax.axis_size("mp")
    mp_here = lax.axis_index("mp")

    def rows_of(block):
        rows = lax.dynamic_slice_in_dim(w_qkv, block * feats, feats, 0)
        return rows.reshape(feats, 3, heads_here, HD)

    projected = jnp.einsum(
        "tf,fjhd->jhtd", tokens, rows_of(mp_here), preferred_element_type=jnp.float32
    )
    for step in range(1, mp_count):
        source = (mp_here - step) % mp_count
        projected = projected + jnp.einsum(
            "tf,fjhd->jhtd",
            passed_along(tokens, "mp", step),
            rows_of(source),
            preferred_element_type=jnp.float32,
        )
    key_norm = lax.rsqrt(jnp.mean(projected[1] * projected[1], axis=-1, keepdims=True) + 1e-06)
    key_part = (projected[1] * key_norm * k_gain).astype(jnp.bfloat16)
    value_part = projected[2].astype(jnp.bfloat16)
    paired = jnp.stack([key_part, value_part])
    position = lax.axis_index("seq")
    seq_count = lax.axis_size("seq")
    core = position % 2
    partner = [(source, source ^ 1) for source in range(seq_count)]
    from_m4 = passed_along(paired, "seq", 4)
    from_m2 = passed_along(paired, "seq", 2)
    from_p2 = passed_along(paired, "seq", -2)
    from_p4 = passed_along(paired, "seq", -4)
    fwd_own = lax.ppermute(paired, "seq", partner)
    fwd_a = lax.ppermute(from_m2, "seq", partner)
    fwd_b = lax.ppermute(from_p2, "seq", partner)
    fwd_c = lax.ppermute(jnp.where(core == 0, from_p4, from_m4), "seq", partner)
    kv_tiles = [paired, from_m4, from_m2, from_p2, from_p4, fwd_own, fwd_a, fwd_b, fwd_c]
    odd = core == 1
    slot_offsets = jnp.stack(
        [
            jnp.int32(0),
            jnp.int32(-4),
            jnp.int32(-2),
            jnp.int32(2),
            jnp.int32(4),
            jnp.where(odd, -1, 1).astype(jnp.int32),
            jnp.where(odd, -3, -1).astype(jnp.int32),
            jnp.where(odd, 1, 3).astype(jnp.int32),
            jnp.where(odd, 3, -3).astype(jnp.int32),
        ]
    )
    slot_tile = jnp.mod(position + slot_offsets, total_tiles)
    listed = lax.dynamic_slice_in_dim(neighbours, position, 1, 0)
    used_counts = lax.dynamic_slice_in_dim(counts, position, 1, 0)
    slot_used = jnp.arange(NB, dtype=jnp.int32)[None, :] < used_counts[:, None]
    hits = (listed[:, :, None] == slot_tile[None, None, :]) & slot_used[:, :, None]
    tile_mask = jnp.any(hits, axis=1)[0].astype(jnp.int32)
    q_raw = projected[0]
    attended = attend(tile_mask, q_raw, q_gain, kv_tiles)
    out_cols = w_out.shape[1] // mp_count
    total = jnp.dot(
        attended,
        lax.dynamic_slice_in_dim(w_out, mp_here * out_cols, out_cols, 1),
        preferred_element_type=jnp.float32,
    ).astype(jnp.bfloat16).astype(jnp.float32)
    for step in range(1, mp_count):
        target = (mp_here + step) % mp_count
        term = jnp.dot(
            attended,
            lax.dynamic_slice_in_dim(w_out, target * out_cols, out_cols, 1),
            preferred_element_type=jnp.float32,
        ).astype(jnp.bfloat16)
        total = total + passed_along(term, "mp", step).astype(jnp.float32)
    return total.astype(jnp.bfloat16)


def solution(mesh):
    return jax.shard_map(
        on_device,
        mesh=mesh,
        in_specs=(P("seq", "mp"), P(None, None, "mp"), P(), P(), P("mp", None), P(), P()),
        out_specs=P("seq", "mp"),
        check_vma=False,
    )
```

```python
import jax
import jax.numpy as jnp
from jax import lax
from jax.experimental import pallas as pl
from jax.experimental.pallas import tpu as pltpu
from jax.sharding import PartitionSpec as P

HD = 128
TILE = 384
REACH = 4
NB = 6


def passed_along(value, axis, steps):
    count = lax.axis_size(axis)
    pairs = [(source, (source + steps) % count) for source in range(count)]
    return lax.ppermute(value, axis, pairs)


def head_norm(projected, gain_vec):
    per_head = projected.reshape(projected.shape[0], -1, HD)
    factor = lax.rsqrt(jnp.mean(per_head * per_head, axis=-1, keepdims=True) + 1e-06)
    return (per_head * factor * gain_vec).astype(jnp.bfloat16)


def attend_kernel(mask_ref, q_ref, gain_ref, *rest):
    slots = len(rest) - 4
    kv_refs = rest[:slots]
    out_ref = rest[slots]
    m_ref, l_ref, acc_ref = rest[slots + 1 :]
    factor = HD ** (-0.5)
    q_raw = q_ref[...]
    norm = lax.rsqrt(jnp.mean(q_raw * q_raw, axis=-1, keepdims=True) + 1e-06)
    q = (q_raw * norm * gain_ref[...]).astype(jnp.bfloat16)
    m_ref[...] = jnp.full(m_ref.shape, -jnp.inf, jnp.float32)
    l_ref[...] = jnp.zeros(l_ref.shape, jnp.float32)
    acc_ref[...] = jnp.zeros(acc_ref.shape, jnp.float32)

    def scores_of(i):
        return lax.dot_general(
            q, kv_refs[i][0], (((1,), (1,)), ((), ())), preferred_element_type=jnp.float32
        )

    for i in range(slots):
        @pl.when(mask_ref[i] > 0)
        def _():
            m_ref[...] = jnp.maximum(m_ref[...], scores_of(i))
    highest = jnp.max(m_ref[...], axis=-1, keepdims=True)
    for i in range(slots):
        @pl.when(mask_ref[i] > 0)
        def _():
            p = jnp.exp((scores_of(i) - highest) * factor)
            l_ref[...] = l_ref[...] + p
            acc_ref[...] = acc_ref[...] + jnp.dot(
                p.astype(jnp.bfloat16), kv_refs[i][1], preferred_element_type=jnp.float32
            )
    total = jnp.sum(l_ref[...], axis=-1, keepdims=True)
    out_ref[...] = (acc_ref[...] / total).astype(jnp.bfloat16)


def attend(slot_mask, q_raw, q_gain, kv_tiles):
    rows, columns = q_raw.shape
    heads = columns // HD
    keys = kv_tiles[0].shape[2]
    slots = len(kv_tiles)
    kv_spec = pl.BlockSpec((2, None, keys, HD), lambda h, mask: (0, h, 0, 0))
    return pl.pallas_call(
        attend_kernel,
        grid_spec=pltpu.PrefetchScalarGridSpec(
            num_scalar_prefetch=1,
            grid=(heads,),
            in_specs=[
                pl.BlockSpec((rows, HD), lambda h, mask: (0, h)),
                pl.BlockSpec((1, HD), lambda h, mask: (0, 0)),
            ]
            + [kv_spec] * slots,
            out_specs=pl.BlockSpec((rows, HD), lambda h, mask: (0, h)),
            scratch_shapes=[
                pltpu.VMEM((rows, keys), jnp.float32),
                pltpu.VMEM((rows, keys), jnp.float32),
                pltpu.VMEM((rows, HD), jnp.float32),
            ],
        ),
        out_shape=jax.ShapeDtypeStruct((rows, columns), jnp.bfloat16),
    )(slot_mask, q_raw, q_gain.reshape(1, HD), *kv_tiles)


def on_device(tokens, w_qkv, q_gain, k_gain, w_out, neighbours, counts):
    tok_rows = tokens.shape[0]
    columns = w_qkv.shape[2]
    heads_here = columns // HD
    tiles_here = tok_rows // TILE
    total_tiles = neighbours.shape[0]
    feats = tokens.shape[1]
    mp_count = lax.axis_size("mp")
    mp_here = lax.axis_index("mp")

    def rows_of(block):
        return lax.dynamic_slice_in_dim(w_qkv, block * feats, feats, 0)

    projected = jnp.einsum(
        "tf,fjc->jtc", tokens, rows_of(mp_here), preferred_element_type=jnp.float32
    )
    for step in range(1, mp_count):
        source = (mp_here - step) % mp_count
        projected = projected + jnp.einsum(
            "tf,fjc->jtc",
            passed_along(tokens, "mp", step),
            rows_of(source),
            preferred_element_type=jnp.float32,
        )
    key_part = head_norm(projected[1], k_gain).transpose(1, 0, 2)
    value_part = projected[2].astype(jnp.bfloat16).reshape(tok_rows, heads_here, HD).transpose(1, 0, 2)
    paired = jnp.stack([key_part, value_part])
    position = lax.axis_index("seq")
    seq_count = lax.axis_size("seq")
    core = position % 2
    partner = [(source, source ^ 1) for source in range(seq_count)]
    from_m4 = passed_along(paired, "seq", 4)
    from_m2 = passed_along(paired, "seq", 2)
    from_p2 = passed_along(paired, "seq", -2)
    from_p4 = passed_along(paired, "seq", -4)
    fwd_own = lax.ppermute(paired, "seq", partner)
    fwd_a = lax.ppermute(from_m2, "seq", partner)
    fwd_b = lax.ppermute(from_p2, "seq", partner)
    fwd_c = lax.ppermute(jnp.where(core == 0, from_p4, from_m4), "seq", partner)
    kv_tiles = [paired, from_m4, from_m2, from_p2, from_p4, fwd_own, fwd_a, fwd_b, fwd_c]
    odd = core == 1
    slot_offsets = jnp.stack(
        [
            jnp.int32(0),
            jnp.int32(-4),
            jnp.int32(-2),
            jnp.int32(2),
            jnp.int32(4),
            jnp.where(odd, -1, 1).astype(jnp.int32),
            jnp.where(odd, -3, -1).astype(jnp.int32),
            jnp.where(odd, 1, 3).astype(jnp.int32),
            jnp.where(odd, 3, -3).astype(jnp.int32),
        ]
    )
    slot_tile = jnp.mod(position + slot_offsets, total_tiles)
    listed = lax.dynamic_slice_in_dim(neighbours, position, 1, 0)
    used_counts = lax.dynamic_slice_in_dim(counts, position, 1, 0)
    slot_used = jnp.arange(NB, dtype=jnp.int32)[None, :] < used_counts[:, None]
    hits = (listed[:, :, None] == slot_tile[None, None, :]) & slot_used[:, :, None]
    tile_mask = jnp.any(hits, axis=1)[0].astype(jnp.int32)
    q_raw = projected[0]
    attended = attend(tile_mask, q_raw, q_gain, kv_tiles)
    out_cols = w_out.shape[1] // mp_count
    total = jnp.dot(
        attended,
        lax.dynamic_slice_in_dim(w_out, mp_here * out_cols, out_cols, 1),
        preferred_element_type=jnp.float32,
    ).astype(jnp.bfloat16).astype(jnp.float32)
    for step in range(1, mp_count):
        target = (mp_here + step) % mp_count
        term = jnp.dot(
            attended,
            lax.dynamic_slice_in_dim(w_out, target * out_cols, out_cols, 1),
            preferred_element_type=jnp.float32,
        ).astype(jnp.bfloat16)
        total = total + passed_along(term, "mp", step).astype(jnp.float32)
    return total.astype(jnp.bfloat16)


def solution(mesh):
    return jax.shard_map(
        on_device,
        mesh=mesh,
        in_specs=(P("seq", "mp"), P(None, None, "mp"), P(), P(), P("mp", None), P(), P()),
        out_specs=P("seq", "mp"),
        check_vma=False,
    )
```

```python
import jax
import jax.numpy as jnp
from jax import lax
from jax.experimental import pallas as pl
from jax.experimental.pallas import tpu as pltpu
from jax.sharding import PartitionSpec as P

HD = 128
TILE = 384
REACH = 4
NB = 6


def passed_along(value, axis, steps):
    count = lax.axis_size(axis)
    pairs = [(source, (source + steps) % count) for source in range(count)]
    return lax.ppermute(value, axis, pairs)


def head_norm(projected, gain_vec):
    per_head = projected.reshape(projected.shape[0], -1, HD)
    factor = lax.rsqrt(jnp.mean(per_head * per_head, axis=-1, keepdims=True) + 1e-06)
    return (per_head * factor * gain_vec).astype(jnp.bfloat16)


def attend_kernel(mask_ref, q_ref, gain_ref, *rest):
    slots = len(rest) - 4
    kv_refs = rest[:slots]
    out_ref = rest[slots]
    m_ref, l_ref, acc_ref = rest[slots + 1 :]
    factor = HD ** (-0.5)
    q_raw = q_ref[...]
    norm = lax.rsqrt(jnp.mean(q_raw * q_raw, axis=-1, keepdims=True) + 1e-06)
    q = (q_raw * norm * gain_ref[...]).astype(jnp.bfloat16)
    m_ref[...] = jnp.full(m_ref.shape, -jnp.inf, jnp.float32)
    l_ref[...] = jnp.zeros(l_ref.shape, jnp.float32)
    acc_ref[...] = jnp.zeros(acc_ref.shape, jnp.float32)

    def scores_of(i):
        return lax.dot_general(
            q, kv_refs[i][0], (((1,), (1,)), ((), ())), preferred_element_type=jnp.float32
        )

    for i in range(slots):
        @pl.when(mask_ref[i] > 0)
        def _():
            m_ref[...] = jnp.maximum(m_ref[...], scores_of(i))
    highest = jnp.max(m_ref[...], axis=-1, keepdims=True)
    for i in range(slots):
        @pl.when(mask_ref[i] > 0)
        def _():
            p = jnp.exp((scores_of(i) - highest) * factor)
            l_ref[...] = l_ref[...] + p
            acc_ref[...] = acc_ref[...] + jnp.dot(
                p.astype(jnp.bfloat16), kv_refs[i][1], preferred_element_type=jnp.float32
            )
    total = jnp.sum(l_ref[...], axis=-1, keepdims=True)
    out_ref[...] = (acc_ref[...] / total).astype(jnp.bfloat16)


def attend(slot_mask, q_raw, q_gain, kv_tiles):
    rows, columns = q_raw.shape
    heads = columns // HD
    keys = kv_tiles[0].shape[2]
    slots = len(kv_tiles)
    kv_spec = pl.BlockSpec((2, None, keys, HD), lambda h, mask: (0, h, 0, 0))
    return pl.pallas_call(
        attend_kernel,
        grid_spec=pltpu.PrefetchScalarGridSpec(
            num_scalar_prefetch=1,
            grid=(heads,),
            in_specs=[
                pl.BlockSpec((rows, HD), lambda h, mask: (0, h)),
                pl.BlockSpec((1, HD), lambda h, mask: (0, 0)),
            ]
            + [kv_spec] * slots,
            out_specs=pl.BlockSpec((rows, HD), lambda h, mask: (0, h)),
            scratch_shapes=[
                pltpu.VMEM((rows, keys), jnp.float32),
                pltpu.VMEM((rows, keys), jnp.float32),
                pltpu.VMEM((rows, HD), jnp.float32),
            ],
        ),
        out_shape=jax.ShapeDtypeStruct((rows, columns), jnp.bfloat16),
    )(slot_mask, q_raw, q_gain.reshape(1, HD), *kv_tiles)


def on_device(tokens, w_qkv, q_gain, k_gain, w_out, neighbours, counts):
    tok_rows = tokens.shape[0]
    columns = w_qkv.shape[2]
    heads_here = columns // HD
    tiles_here = tok_rows // TILE
    total_tiles = neighbours.shape[0]
    feats = tokens.shape[1]
    mp_count = lax.axis_size("mp")
    mp_here = lax.axis_index("mp")

    def rows_of(block):
        return lax.dynamic_slice_in_dim(w_qkv, block * feats, feats, 0)

    position = lax.axis_index("seq")
    seq_count = lax.axis_size("seq")
    core = position % 2
    odd = core == 1
    slot_offsets = jnp.stack(
        [
            jnp.int32(0),
            jnp.int32(-4),
            jnp.int32(-2),
            jnp.int32(2),
            jnp.int32(4),
            jnp.where(odd, -1, 1).astype(jnp.int32),
            jnp.where(odd, -3, -1).astype(jnp.int32),
            jnp.where(odd, 1, 3).astype(jnp.int32),
            jnp.int32(-3),
            jnp.int32(3),
        ]
    )
    slot_tile = jnp.mod(position + slot_offsets, total_tiles)
    slot_tile = slot_tile.at[8].set(jnp.where(odd, -1, slot_tile[8]))
    slot_tile = slot_tile.at[9].set(jnp.where(odd, slot_tile[9], -1))
    listed = lax.dynamic_slice_in_dim(neighbours, position, 1, 0)
    used_counts = lax.dynamic_slice_in_dim(counts, position, 1, 0)
    slot_used = jnp.arange(NB, dtype=jnp.int32)[None, :] < used_counts[:, None]
    hits = (listed[:, :, None] == slot_tile[None, None, :]) & slot_used[:, :, None]
    tile_mask = jnp.any(hits, axis=1)[0].astype(jnp.int32)
    projected = jnp.einsum(
        "tf,fjc->jtc", tokens, rows_of(mp_here), preferred_element_type=jnp.float32
    )
    projected, tile_mask = lax.optimization_barrier((projected, tile_mask))
    for step in range(1, mp_count):
        source = (mp_here - step) % mp_count
        projected = projected + jnp.einsum(
            "tf,fjc->jtc",
            passed_along(tokens, "mp", step),
            rows_of(source),
            preferred_element_type=jnp.float32,
        )
    key_part = head_norm(projected[1], k_gain).transpose(1, 0, 2)
    value_part = projected[2].astype(jnp.bfloat16).reshape(tok_rows, heads_here, HD).transpose(1, 0, 2)
    paired = jnp.stack([key_part, value_part])
    partner = [(source, source ^ 1) for source in range(seq_count)]
    from_m4 = passed_along(paired, "seq", 4)
    from_m2 = passed_along(paired, "seq", 2)
    from_p2 = passed_along(paired, "seq", -2)
    from_p4 = passed_along(paired, "seq", -4)
    fwd_own = lax.ppermute(paired, "seq", partner)
    fwd_a = lax.ppermute(from_m2, "seq", partner)
    fwd_b = lax.ppermute(from_p2, "seq", partner)
    even_to_odd = [(source, source ^ 1) for source in range(0, seq_count, 2)]
    odd_to_even = [(source, source ^ 1) for source in range(1, seq_count, 2)]
    fwd_even = lax.ppermute(from_m4, "seq", odd_to_even)
    fwd_odd = lax.ppermute(from_p4, "seq", even_to_odd)
    kv_tiles = [paired, from_m4, from_m2, from_p2, from_p4, fwd_own, fwd_a, fwd_b, fwd_even, fwd_odd]
    q_raw = projected[0]
    attended = attend(tile_mask, q_raw, q_gain, kv_tiles)
    out_cols = w_out.shape[1] // mp_count
    total = jnp.dot(
        attended,
        lax.dynamic_slice_in_dim(w_out, mp_here * out_cols, out_cols, 1),
        preferred_element_type=jnp.float32,
    ).astype(jnp.bfloat16).astype(jnp.float32)
    for step in range(1, mp_count):
        target = (mp_here + step) % mp_count
        term = jnp.dot(
            attended,
            lax.dynamic_slice_in_dim(w_out, target * out_cols, out_cols, 1),
            preferred_element_type=jnp.float32,
        ).astype(jnp.bfloat16)
        total = total + passed_along(term, "mp", step).astype(jnp.float32)
    return total.astype(jnp.bfloat16)


def solution(mesh):
    return jax.shard_map(
        on_device,
        mesh=mesh,
        in_specs=(P("seq", "mp"), P(None, None, "mp"), P(), P(), P("mp", None), P(), P()),
        out_specs=P("seq", "mp"),
        check_vma=False,
    )
```

```python
import jax
import jax.numpy as jnp
from jax import lax
from jax.experimental import pallas as pl
from jax.experimental.pallas import tpu as pltpu
from jax.sharding import PartitionSpec as P

HD = 128
TILE = 384
REACH = 4
NB = 6


def passed_along(value, axis, steps):
    count = lax.axis_size(axis)
    pairs = [(source, (source + steps) % count) for source in range(count)]
    return lax.ppermute(value, axis, pairs)


def head_norm(projected, gain_vec):
    per_head = projected.reshape(projected.shape[0], -1, HD)
    factor = lax.rsqrt(jnp.mean(per_head * per_head, axis=-1, keepdims=True) + 1e-06)
    return (per_head * factor * gain_vec).astype(jnp.bfloat16)


def attend_kernel(mask_ref, q_ref, gain_ref, *rest):
    slots = len(rest) - 4
    kv_refs = rest[:slots]
    out_ref = rest[slots]
    m_ref, l_ref, acc_ref = rest[slots + 1 :]
    factor = HD ** (-0.5)
    q_raw = q_ref[...]
    norm = lax.rsqrt(jnp.mean(q_raw * q_raw, axis=-1, keepdims=True) + 1e-06)
    q = (q_raw * norm * gain_ref[...]).astype(jnp.bfloat16)
    m_ref[...] = jnp.full(m_ref.shape, -jnp.inf, jnp.float32)
    l_ref[...] = jnp.zeros(l_ref.shape, jnp.float32)
    acc_ref[...] = jnp.zeros(acc_ref.shape, jnp.float32)

    def scores_of(i):
        return lax.dot_general(
            q, kv_refs[i][0], (((1,), (1,)), ((), ())), preferred_element_type=jnp.float32
        )

    for i in range(slots):
        @pl.when(mask_ref[i] > 0)
        def _():
            m_ref[...] = jnp.maximum(m_ref[...], scores_of(i))
    highest = jnp.max(m_ref[...], axis=-1, keepdims=True)
    for i in range(slots):
        @pl.when(mask_ref[i] > 0)
        def _():
            p = jnp.exp((scores_of(i) - highest) * factor)
            l_ref[...] = l_ref[...] + p
            acc_ref[...] = acc_ref[...] + jnp.dot(
                p.astype(jnp.bfloat16), kv_refs[i][1], preferred_element_type=jnp.float32
            )
    total = jnp.sum(l_ref[...], axis=-1, keepdims=True)
    out_ref[...] = (acc_ref[...] / total).astype(jnp.bfloat16)


def attend(slot_mask, q_raw, q_gain, kv_tiles):
    rows, columns = q_raw.shape
    heads = columns // HD
    keys = kv_tiles[0].shape[2]
    slots = len(kv_tiles)
    kv_spec = pl.BlockSpec((2, None, keys, HD), lambda h, mask: (0, h, 0, 0))
    return pl.pallas_call(
        attend_kernel,
        grid_spec=pltpu.PrefetchScalarGridSpec(
            num_scalar_prefetch=1,
            grid=(heads,),
            in_specs=[
                pl.BlockSpec((rows, HD), lambda h, mask: (0, h)),
                pl.BlockSpec((1, HD), lambda h, mask: (0, 0)),
            ]
            + [kv_spec] * slots,
            out_specs=pl.BlockSpec((rows, HD), lambda h, mask: (0, h)),
            scratch_shapes=[
                pltpu.VMEM((rows, keys), jnp.float32),
                pltpu.VMEM((rows, keys), jnp.float32),
                pltpu.VMEM((rows, HD), jnp.float32),
            ],
        ),
        out_shape=jax.ShapeDtypeStruct((rows, columns), jnp.bfloat16),
    )(slot_mask, q_raw, q_gain.reshape(1, HD), *kv_tiles)


def on_device(tokens, w_qkv, q_gain, k_gain, w_out, neighbours, counts):
    tok_rows = tokens.shape[0]
    columns = w_qkv.shape[2]
    heads_here = columns // HD
    tiles_here = tok_rows // TILE
    total_tiles = neighbours.shape[0]
    feats = tokens.shape[1]
    mp_count = lax.axis_size("mp")
    mp_here = lax.axis_index("mp")

    def rows_of(block):
        return lax.dynamic_slice_in_dim(w_qkv, block * feats, feats, 0)

    projected = jnp.einsum(
        "tf,fjc->jtc", tokens, rows_of(mp_here), preferred_element_type=jnp.float32
    )
    for step in range(1, mp_count):
        source = (mp_here - step) % mp_count
        projected = projected + jnp.einsum(
            "tf,fjc->jtc",
            passed_along(tokens, "mp", step),
            rows_of(source),
            preferred_element_type=jnp.float32,
        )
    key_part = head_norm(projected[1], k_gain).transpose(1, 0, 2)
    value_part = projected[2].astype(jnp.bfloat16).reshape(tok_rows, heads_here, HD).transpose(1, 0, 2)
    paired = jnp.stack([key_part, value_part])
    position = lax.axis_index("seq")
    seq_count = lax.axis_size("seq")
    core = position % 2
    partner = [(source, source ^ 1) for source in range(seq_count)]
    from_m4 = passed_along(paired, "seq", 4)
    from_m2 = passed_along(paired, "seq", 2)
    from_p2 = passed_along(paired, "seq", -2)
    from_p4 = passed_along(paired, "seq", -4)
    fwd_own = lax.ppermute(paired, "seq", partner)
    fwd_a = lax.ppermute(from_m2, "seq", partner)
    fwd_b = lax.ppermute(from_p2, "seq", partner)
    fwd_c = lax.ppermute(jnp.where(core == 0, from_p4, from_m4), "seq", partner)
    kv_tiles = [paired, from_m4, from_m2, from_p2, from_p4, fwd_own, fwd_a, fwd_b, fwd_c]
    odd = core == 1
    slot_offsets = jnp.stack(
        [
            jnp.int32(0),
            jnp.int32(-4),
            jnp.int32(-2),
            jnp.int32(2),
            jnp.int32(4),
            jnp.where(odd, -1, 1).astype(jnp.int32),
            jnp.where(odd, -3, -1).astype(jnp.int32),
            jnp.where(odd, 1, 3).astype(jnp.int32),
            jnp.where(odd, 3, -3).astype(jnp.int32),
        ]
    )
    slot_tile = jnp.mod(position + slot_offsets, total_tiles)
    listed = lax.dynamic_slice_in_dim(neighbours, position, 1, 0)
    used_counts = lax.dynamic_slice_in_dim(counts, position, 1, 0)
    slot_used = jnp.arange(NB, dtype=jnp.int32)[None, :] < used_counts[:, None]
    hits = (listed[:, :, None] == slot_tile[None, None, :]) & slot_used[:, :, None]
    tile_mask = jnp.any(hits, axis=1)[0].astype(jnp.int32)
    q_raw = projected[0]
    attended = attend(tile_mask, q_raw, q_gain, kv_tiles)
    out_cols = w_out.shape[1] // mp_count
    terms = jnp.dot(attended, w_out, preferred_element_type=jnp.float32).astype(jnp.bfloat16)
    terms = terms.reshape(tok_rows, mp_count, out_cols).transpose(1, 0, 2)
    total = lax.dynamic_index_in_dim(terms, mp_here, 0, keepdims=False).astype(jnp.float32)
    for step in range(1, mp_count):
        target = (mp_here + step) % mp_count
        term = lax.dynamic_index_in_dim(terms, target, 0, keepdims=False)
        total = total + passed_along(term, "mp", step).astype(jnp.float32)
    return total.astype(jnp.bfloat16)


def solution(mesh):
    return jax.shard_map(
        on_device,
        mesh=mesh,
        in_specs=(P("seq", "mp"), P(None, None, "mp"), P(), P(), P("mp", None), P(), P()),
        out_specs=P("seq", "mp"),
        check_vma=False,
    )
```

```python
import jax
import jax.numpy as jnp
from jax import lax
from jax.experimental import pallas as pl
from jax.experimental.pallas import tpu as pltpu
from jax.sharding import PartitionSpec as P

HD = 128
TILE = 384
REACH = 4
NB = 6


def passed_along(value, axis, steps):
    count = lax.axis_size(axis)
    pairs = [(source, (source + steps) % count) for source in range(count)]
    return lax.ppermute(value, axis, pairs)


def head_norm(projected, gain_vec):
    per_head = projected.reshape(projected.shape[0], -1, HD)
    factor = lax.rsqrt(jnp.mean(per_head * per_head, axis=-1, keepdims=True) + 1e-06)
    return (per_head * factor * gain_vec).astype(jnp.bfloat16)


def attend_kernel(mask_ref, q_ref, gain_ref, *rest):
    slots = len(rest) - 4
    kv_refs = rest[:slots]
    out_ref = rest[slots]
    m_ref, l_ref, acc_ref = rest[slots + 1 :]
    factor = HD ** (-0.5)
    q_raw = q_ref[...]
    norm = lax.rsqrt(jnp.mean(q_raw * q_raw, axis=-1, keepdims=True) + 1e-06)
    q = (q_raw * norm * gain_ref[...]).astype(jnp.bfloat16)
    m_ref[...] = jnp.full(m_ref.shape, -jnp.inf, jnp.float32)
    l_ref[...] = jnp.zeros(l_ref.shape, jnp.float32)
    acc_ref[...] = jnp.zeros(acc_ref.shape, jnp.float32)

    def scores_of(i):
        return lax.dot_general(
            q, kv_refs[i][0], (((1,), (1,)), ((), ())), preferred_element_type=jnp.float32
        )

    for i in range(slots):
        @pl.when(mask_ref[i] > 0)
        def _():
            m_ref[...] = jnp.maximum(m_ref[...], scores_of(i))
    highest = jnp.max(m_ref[...], axis=-1, keepdims=True)
    for i in range(slots):
        @pl.when(mask_ref[i] > 0)
        def _():
            p = jnp.exp((scores_of(i) - highest) * factor)
            l_ref[...] = l_ref[...] + p
            acc_ref[...] = acc_ref[...] + jnp.dot(
                p.astype(jnp.bfloat16), kv_refs[i][1], preferred_element_type=jnp.float32
            )
    total = jnp.sum(l_ref[...], axis=-1, keepdims=True)
    out_ref[...] = (acc_ref[...] / total).astype(jnp.bfloat16)


def attend(slot_mask, q_raw, q_gain, kv_tiles):
    rows, columns = q_raw.shape
    heads = columns // HD
    keys = kv_tiles[0].shape[2]
    slots = len(kv_tiles)
    kv_spec = pl.BlockSpec((2, None, keys, HD), lambda h, mask: (0, h, 0, 0))
    return pl.pallas_call(
        attend_kernel,
        grid_spec=pltpu.PrefetchScalarGridSpec(
            num_scalar_prefetch=1,
            grid=(heads,),
            in_specs=[
                pl.BlockSpec((rows, HD), lambda h, mask: (0, h)),
                pl.BlockSpec((1, HD), lambda h, mask: (0, 0)),
            ]
            + [kv_spec] * slots,
            out_specs=pl.BlockSpec((rows, HD), lambda h, mask: (0, h)),
            scratch_shapes=[
                pltpu.VMEM((rows, keys), jnp.float32),
                pltpu.VMEM((rows, keys), jnp.float32),
                pltpu.VMEM((rows, HD), jnp.float32),
            ],
        ),
        out_shape=jax.ShapeDtypeStruct((rows, columns), jnp.bfloat16),
    )(slot_mask, q_raw, q_gain.reshape(1, HD), *kv_tiles)


def on_device(tokens, w_qkv, q_gain, k_gain, w_out, neighbours, counts):
    tok_rows = tokens.shape[0]
    columns = w_qkv.shape[2]
    heads_here = columns // HD
    tiles_here = tok_rows // TILE
    total_tiles = neighbours.shape[0]
    feats = tokens.shape[1]
    mp_count = lax.axis_size("mp")
    mp_here = lax.axis_index("mp")

    def rows_of(block):
        return lax.dynamic_slice_in_dim(w_qkv, block * feats, feats, 0)

    projected = jnp.einsum(
        "tf,fjc->jtc", tokens, rows_of(mp_here), preferred_element_type=jnp.float32
    )
    for step in range(1, mp_count):
        source = (mp_here - step) % mp_count
        projected = projected + jnp.einsum(
            "tf,fjc->jtc",
            passed_along(tokens, "mp", step),
            rows_of(source),
            preferred_element_type=jnp.float32,
        )
    key_part = head_norm(projected[1], k_gain).transpose(1, 0, 2)
    value_part = projected[2].astype(jnp.bfloat16).reshape(tok_rows, heads_here, HD).transpose(1, 0, 2)
    paired = jnp.stack([key_part, value_part])
    position = lax.axis_index("seq")
    seq_count = lax.axis_size("seq")
    core = position % 2
    partner = [(source, source ^ 1) for source in range(seq_count)]
    from_m4 = passed_along(paired, "seq", 4)
    from_m2 = passed_along(paired, "seq", 2)
    from_p2 = passed_along(paired, "seq", -2)
    from_p4 = passed_along(paired, "seq", -4)
    fwd_own = lax.ppermute(paired, "seq", partner)
    fwd_a = lax.ppermute(from_m2, "seq", partner)
    fwd_b = lax.ppermute(from_p2, "seq", partner)
    fwd_c = lax.ppermute(jnp.where(core == 0, from_p4, from_m4), "seq", partner)
    kv_tiles = [paired, from_m4, from_m2, from_p2, from_p4, fwd_own, fwd_a, fwd_b, fwd_c]
    odd = core == 1
    slot_offsets = jnp.stack(
        [
            jnp.int32(0),
            jnp.int32(-4),
            jnp.int32(-2),
            jnp.int32(2),
            jnp.int32(4),
            jnp.where(odd, -1, 1).astype(jnp.int32),
            jnp.where(odd, -3, -1).astype(jnp.int32),
            jnp.where(odd, 1, 3).astype(jnp.int32),
            jnp.where(odd, 3, -3).astype(jnp.int32),
        ]
    )
    slot_tile = jnp.mod(position + slot_offsets, total_tiles)
    listed = lax.dynamic_slice_in_dim(neighbours, position, 1, 0)
    used_counts = lax.dynamic_slice_in_dim(counts, position, 1, 0)
    slot_used = jnp.arange(NB, dtype=jnp.int32)[None, :] < used_counts[:, None]
    hits = (listed[:, :, None] == slot_tile[None, None, :]) & slot_used[:, :, None]
    tile_mask = jnp.any(hits, axis=1)[0].astype(jnp.int32)
    q_raw = projected[0]
    attended = attend(tile_mask, q_raw, q_gain, kv_tiles)
    out_cols = w_out.shape[1] // mp_count
    terms = jnp.einsum(
        "tk,kjc->jtc",
        attended,
        w_out.reshape(w_out.shape[0], mp_count, out_cols),
        preferred_element_type=jnp.float32,
    ).astype(jnp.bfloat16)
    total = lax.dynamic_index_in_dim(terms, mp_here, 0, keepdims=False).astype(jnp.float32)
    for step in range(1, mp_count):
        target = (mp_here + step) % mp_count
        term = lax.dynamic_index_in_dim(terms, target, 0, keepdims=False)
        total = total + passed_along(term, "mp", step).astype(jnp.float32)
    return total.astype(jnp.bfloat16)


def solution(mesh):
    return jax.shard_map(
        on_device,
        mesh=mesh,
        in_specs=(P("seq", "mp"), P(None, None, "mp"), P(), P(), P("mp", None), P(), P()),
        out_specs=P("seq", "mp"),
        check_vma=False,
    )
```

```python
import jax
import jax.numpy as jnp
from jax import lax
from jax.experimental import pallas as pl
from jax.experimental.pallas import tpu as pltpu
from jax.sharding import PartitionSpec as P

HD = 128
TILE = 384
REACH = 4
NB = 6


def passed_along(value, axis, steps):
    count = lax.axis_size(axis)
    pairs = [(source, (source + steps) % count) for source in range(count)]
    return lax.ppermute(value, axis, pairs)


def head_norm(projected, gain_vec):
    per_head = projected.reshape(projected.shape[0], -1, HD)
    factor = lax.rsqrt(jnp.mean(per_head * per_head, axis=-1, keepdims=True) + 1e-06)
    return (per_head * factor * gain_vec).astype(jnp.bfloat16)


def attend_kernel(mask_ref, q_ref, gain_ref, *rest):
    slots = len(rest) - 4
    kv_refs = rest[:slots]
    out_ref = rest[slots]
    m_ref, l_ref, acc_ref = rest[slots + 1 :]
    factor = HD ** (-0.5)
    q_raw = q_ref[...]
    norm = lax.rsqrt(jnp.mean(q_raw * q_raw, axis=-1, keepdims=True) + 1e-06)
    q = (q_raw * norm * gain_ref[...]).astype(jnp.bfloat16)
    m_ref[...] = jnp.full(m_ref.shape, -jnp.inf, jnp.float32)
    l_ref[...] = jnp.zeros(l_ref.shape, jnp.float32)
    acc_ref[...] = jnp.zeros(acc_ref.shape, jnp.float32)

    def scores_of(i):
        return lax.dot_general(
            q, kv_refs[i][0], (((1,), (1,)), ((), ())), preferred_element_type=jnp.float32
        )

    for i in range(slots):
        @pl.when(mask_ref[i] > 0)
        def _():
            m_ref[...] = jnp.maximum(m_ref[...], scores_of(i))
    highest = jnp.max(m_ref[...], axis=-1, keepdims=True)
    for i in range(slots):
        @pl.when(mask_ref[i] > 0)
        def _():
            p = jnp.exp((scores_of(i) - highest) * factor)
            l_ref[...] = l_ref[...] + p
            acc_ref[...] = acc_ref[...] + jnp.dot(
                p.astype(jnp.bfloat16), kv_refs[i][1], preferred_element_type=jnp.float32
            )
    total = jnp.sum(l_ref[...], axis=-1, keepdims=True)
    out_ref[...] = (acc_ref[...] / total).astype(jnp.bfloat16)


def attend(slot_mask, q_raw, q_gain, kv_tiles):
    rows, columns = q_raw.shape
    heads = columns // HD
    keys = kv_tiles[0].shape[2]
    slots = len(kv_tiles)
    kv_spec = pl.BlockSpec((2, None, keys, HD), lambda h, mask: (0, h, 0, 0))
    return pl.pallas_call(
        attend_kernel,
        grid_spec=pltpu.PrefetchScalarGridSpec(
            num_scalar_prefetch=1,
            grid=(heads,),
            in_specs=[
                pl.BlockSpec((rows, HD), lambda h, mask: (0, h)),
                pl.BlockSpec((1, HD), lambda h, mask: (0, 0)),
            ]
            + [kv_spec] * slots,
            out_specs=pl.BlockSpec((rows, HD), lambda h, mask: (0, h)),
            scratch_shapes=[
                pltpu.VMEM((rows, keys), jnp.float32),
                pltpu.VMEM((rows, keys), jnp.float32),
                pltpu.VMEM((rows, HD), jnp.float32),
            ],
        ),
        out_shape=jax.ShapeDtypeStruct((rows, columns), jnp.bfloat16),
    )(slot_mask, q_raw, q_gain.reshape(1, HD), *kv_tiles)


def on_device(tokens, w_qkv, q_gain, k_gain, w_out, neighbours, counts):
    tok_rows = tokens.shape[0]
    columns = w_qkv.shape[2]
    heads_here = columns // HD
    tiles_here = tok_rows // TILE
    total_tiles = neighbours.shape[0]
    feats = tokens.shape[1]
    mp_count = lax.axis_size("mp")
    mp_here = lax.axis_index("mp")

    def rows_of(block):
        return lax.dynamic_slice_in_dim(w_qkv, block * feats, feats, 0)

    projected = jnp.einsum(
        "tf,fjc->jtc", tokens, rows_of(mp_here), preferred_element_type=jnp.float32
    )
    for step in range(1, mp_count):
        source = (mp_here - step) % mp_count
        projected = projected + jnp.einsum(
            "tf,fjc->jtc",
            passed_along(tokens, "mp", step),
            rows_of(source),
            preferred_element_type=jnp.float32,
        )
    key_part = head_norm(projected[1], k_gain).transpose(1, 0, 2)
    value_part = projected[2].astype(jnp.bfloat16).reshape(tok_rows, heads_here, HD).transpose(1, 0, 2)
    paired = jnp.stack([key_part, value_part])
    position = lax.axis_index("seq")
    seq_count = lax.axis_size("seq")
    core = position % 2
    partner = [(source, source ^ 1) for source in range(seq_count)]
    from_m4 = passed_along(paired, "seq", 4)
    from_m2 = passed_along(paired, "seq", 2)
    from_p2 = passed_along(paired, "seq", -2)
    from_p4 = passed_along(paired, "seq", -4)
    fwd_own = lax.ppermute(paired, "seq", partner)
    fwd_a = lax.ppermute(from_m2, "seq", partner)
    fwd_b = lax.ppermute(from_p2, "seq", partner)
    fwd_c = lax.ppermute(jnp.where(core == 0, from_p4, from_m4), "seq", partner)
    kv_tiles = [paired, from_m4, from_m2, from_p2, from_p4, fwd_own, fwd_a, fwd_b, fwd_c]
    odd = core == 1
    slot_offsets = jnp.stack(
        [
            jnp.int32(0),
            jnp.int32(-4),
            jnp.int32(-2),
            jnp.int32(2),
            jnp.int32(4),
            jnp.where(odd, -1, 1).astype(jnp.int32),
            jnp.where(odd, -3, -1).astype(jnp.int32),
            jnp.where(odd, 1, 3).astype(jnp.int32),
            jnp.where(odd, 3, -3).astype(jnp.int32),
        ]
    )
    slot_tile = jnp.mod(position + slot_offsets, total_tiles)
    listed = lax.dynamic_slice_in_dim(neighbours, position, 1, 0)
    used_counts = lax.dynamic_slice_in_dim(counts, position, 1, 0)
    slot_used = jnp.arange(NB, dtype=jnp.int32)[None, :] < used_counts[:, None]
    hits = (listed[:, :, None] == slot_tile[None, None, :]) & slot_used[:, :, None]
    tile_mask = jnp.any(hits, axis=1)[0].astype(jnp.int32)
    q_raw = projected[0]
    attended = attend(tile_mask, q_raw, q_gain, kv_tiles)
    out_cols = w_out.shape[1] // mp_count
    terms = jnp.einsum(
        "tk,kjc->jtc",
        attended,
        w_out.reshape(w_out.shape[0], mp_count, out_cols),
        preferred_element_type=jnp.float32,
    ).astype(jnp.bfloat16)
    received = lax.all_to_all(terms, "mp", 0, 0, tiled=True).astype(jnp.float32)
    return jnp.sum(received, axis=0).astype(jnp.bfloat16)


def solution(mesh):
    return jax.shard_map(
        on_device,
        mesh=mesh,
        in_specs=(P("seq", "mp"), P(None, None, "mp"), P(), P(), P("mp", None), P(), P()),
        out_specs=P("seq", "mp"),
        check_vma=False,
    )
```

```python
import jax
import jax.numpy as jnp
from jax import lax
from jax.experimental import pallas as pl
from jax.experimental.pallas import tpu as pltpu
from jax.sharding import PartitionSpec as P

HD = 128
TILE = 384
REACH = 4
NB = 6


def passed_along(value, axis, steps):
    count = lax.axis_size(axis)
    pairs = [(source, (source + steps) % count) for source in range(count)]
    return lax.ppermute(value, axis, pairs)


def head_norm(projected, gain_vec):
    per_head = projected.reshape(projected.shape[0], -1, HD)
    factor = lax.rsqrt(jnp.mean(per_head * per_head, axis=-1, keepdims=True) + 1e-06)
    return (per_head * factor * gain_vec).astype(jnp.bfloat16)


def attend_kernel(mask_ref, q_ref, gain_ref, *rest):
    slots = len(rest) - 4
    kv_refs = rest[:slots]
    out_ref = rest[slots]
    m_ref, l_ref, acc_ref = rest[slots + 1 :]
    factor = HD ** (-0.5)
    q_raw = q_ref[...]
    norm = lax.rsqrt(jnp.mean(q_raw * q_raw, axis=-1, keepdims=True) + 1e-06)
    q = (q_raw * norm * gain_ref[...]).astype(jnp.bfloat16)
    m_ref[...] = jnp.full(m_ref.shape, -jnp.inf, jnp.float32)
    l_ref[...] = jnp.zeros(l_ref.shape, jnp.float32)
    acc_ref[...] = jnp.zeros(acc_ref.shape, jnp.float32)

    def scores_of(i):
        return lax.dot_general(
            q, kv_refs[i][0], (((1,), (1,)), ((), ())), preferred_element_type=jnp.float32
        )

    for i in range(slots):
        @pl.when(mask_ref[i] > 0)
        def _():
            m_ref[...] = jnp.maximum(m_ref[...], scores_of(i))
    highest = jnp.max(m_ref[...], axis=-1, keepdims=True)
    for i in range(slots):
        @pl.when(mask_ref[i] > 0)
        def _():
            p = jnp.exp((scores_of(i) - highest) * factor)
            l_ref[...] = l_ref[...] + p
            acc_ref[...] = acc_ref[...] + jnp.dot(
                p.astype(jnp.bfloat16), kv_refs[i][1], preferred_element_type=jnp.float32
            )
    total = jnp.sum(l_ref[...], axis=-1, keepdims=True)
    out_ref[...] = (acc_ref[...] / total).astype(jnp.bfloat16)


def attend(slot_mask, q_raw, q_gain, kv_tiles):
    rows, columns = q_raw.shape
    heads = columns // HD
    keys = kv_tiles[0].shape[2]
    slots = len(kv_tiles)
    kv_spec = pl.BlockSpec((2, None, keys, HD), lambda h, mask: (0, h, 0, 0))
    return pl.pallas_call(
        attend_kernel,
        grid_spec=pltpu.PrefetchScalarGridSpec(
            num_scalar_prefetch=1,
            grid=(heads,),
            in_specs=[
                pl.BlockSpec((rows, HD), lambda h, mask: (0, h)),
                pl.BlockSpec((1, HD), lambda h, mask: (0, 0)),
            ]
            + [kv_spec] * slots,
            out_specs=pl.BlockSpec((rows, HD), lambda h, mask: (0, h)),
            scratch_shapes=[
                pltpu.VMEM((rows, keys), jnp.float32),
                pltpu.VMEM((rows, keys), jnp.float32),
                pltpu.VMEM((rows, HD), jnp.float32),
            ],
        ),
        out_shape=jax.ShapeDtypeStruct((rows, columns), jnp.bfloat16),
    )(slot_mask, q_raw, q_gain.reshape(1, HD), *kv_tiles)


def on_device(tokens, w_qkv, q_gain, k_gain, w_out, neighbours, counts):
    tok_rows = tokens.shape[0]
    columns = w_qkv.shape[2]
    heads_here = columns // HD
    tiles_here = tok_rows // TILE
    total_tiles = neighbours.shape[0]
    feats = tokens.shape[1]
    mp_count = lax.axis_size("mp")
    mp_here = lax.axis_index("mp")

    spread = jnp.broadcast_to(tokens[None], (mp_count,) + tokens.shape)
    gathered = lax.all_to_all(spread, "mp", 0, 0, tiled=True)
    projected = jnp.einsum(
        "itf,ifjc->jtc",
        gathered,
        w_qkv.reshape(mp_count, feats, 3, columns),
        preferred_element_type=jnp.float32,
    )
    key_part = head_norm(projected[1], k_gain).transpose(1, 0, 2)
    value_part = projected[2].astype(jnp.bfloat16).reshape(tok_rows, heads_here, HD).transpose(1, 0, 2)
    paired = jnp.stack([key_part, value_part])
    position = lax.axis_index("seq")
    seq_count = lax.axis_size("seq")
    core = position % 2
    partner = [(source, source ^ 1) for source in range(seq_count)]
    from_m4 = passed_along(paired, "seq", 4)
    from_m2 = passed_along(paired, "seq", 2)
    from_p2 = passed_along(paired, "seq", -2)
    from_p4 = passed_along(paired, "seq", -4)
    fwd_own = lax.ppermute(paired, "seq", partner)
    fwd_a = lax.ppermute(from_m2, "seq", partner)
    fwd_b = lax.ppermute(from_p2, "seq", partner)
    fwd_c = lax.ppermute(jnp.where(core == 0, from_p4, from_m4), "seq", partner)
    kv_tiles = [paired, from_m4, from_m2, from_p2, from_p4, fwd_own, fwd_a, fwd_b, fwd_c]
    odd = core == 1
    slot_offsets = jnp.stack(
        [
            jnp.int32(0),
            jnp.int32(-4),
            jnp.int32(-2),
            jnp.int32(2),
            jnp.int32(4),
            jnp.where(odd, -1, 1).astype(jnp.int32),
            jnp.where(odd, -3, -1).astype(jnp.int32),
            jnp.where(odd, 1, 3).astype(jnp.int32),
            jnp.where(odd, 3, -3).astype(jnp.int32),
        ]
    )
    slot_tile = jnp.mod(position + slot_offsets, total_tiles)
    listed = lax.dynamic_slice_in_dim(neighbours, position, 1, 0)
    used_counts = lax.dynamic_slice_in_dim(counts, position, 1, 0)
    slot_used = jnp.arange(NB, dtype=jnp.int32)[None, :] < used_counts[:, None]
    hits = (listed[:, :, None] == slot_tile[None, None, :]) & slot_used[:, :, None]
    tile_mask = jnp.any(hits, axis=1)[0].astype(jnp.int32)
    q_raw = projected[0]
    attended = attend(tile_mask, q_raw, q_gain, kv_tiles)
    out_cols = w_out.shape[1] // mp_count
    terms = jnp.einsum(
        "tk,kjc->jtc",
        attended,
        w_out.reshape(w_out.shape[0], mp_count, out_cols),
        preferred_element_type=jnp.float32,
    ).astype(jnp.bfloat16)
    received = lax.all_to_all(terms, "mp", 0, 0, tiled=True).astype(jnp.float32)
    return jnp.sum(received, axis=0).astype(jnp.bfloat16)


def solution(mesh):
    return jax.shard_map(
        on_device,
        mesh=mesh,
        in_specs=(P("seq", "mp"), P(None, None, "mp"), P(), P(), P("mp", None), P(), P()),
        out_specs=P("seq", "mp"),
        check_vma=False,
    )
```

```python
import jax
import jax.numpy as jnp
from jax import lax
from jax.experimental import pallas as pl
from jax.experimental.pallas import tpu as pltpu
from jax.sharding import PartitionSpec as P

HD = 128
TILE = 384
REACH = 4
NB = 6


def passed_along(value, axis, steps):
    count = lax.axis_size(axis)
    pairs = [(source, (source + steps) % count) for source in range(count)]
    return lax.ppermute(value, axis, pairs)


def head_norm(projected, gain_vec):
    per_head = projected.reshape(projected.shape[0], -1, HD)
    factor = lax.rsqrt(jnp.mean(per_head * per_head, axis=-1, keepdims=True) + 1e-06)
    return (per_head * factor * gain_vec).astype(jnp.bfloat16)


def attend_kernel(mask_ref, q_ref, gain_ref, *rest):
    slots = len(rest) - 5
    kv_refs = rest[:slots]
    out_ref = rest[slots]
    s_ref, m_ref, l_ref, acc_ref = rest[slots + 1 :]
    factor = HD ** (-0.5)
    q_raw = q_ref[...]
    norm = lax.rsqrt(jnp.mean(q_raw * q_raw, axis=-1, keepdims=True) + 1e-06)
    q = (q_raw * norm * gain_ref[...]).astype(jnp.bfloat16)
    keys = s_ref.shape[2]
    m_ref[...] = jnp.full(m_ref.shape, -jnp.inf, jnp.float32)
    l_ref[...] = jnp.zeros(l_ref.shape, jnp.float32)
    acc_ref[...] = jnp.zeros(acc_ref.shape, jnp.float32)
    for i in range(slots):
        bias = jnp.where(mask_ref[i] > 0, 0.0, -jnp.inf).astype(jnp.float32)
        s = lax.dot_general(
            q, kv_refs[i][0], (((1,), (1,)), ((), ())), preferred_element_type=jnp.float32
        ) + bias
        s_ref[i] = s
        m_ref[...] = jnp.maximum(m_ref[...], s)
    highest = jnp.max(m_ref[...], axis=-1, keepdims=True)
    for i in range(slots):
        p = jnp.exp((s_ref[i] - highest) * factor)
        l_ref[...] = l_ref[...] + p
        acc_ref[...] = acc_ref[...] + jnp.dot(
            p.astype(jnp.bfloat16), kv_refs[i][1], preferred_element_type=jnp.float32
        )
    total = jnp.sum(l_ref[...], axis=-1, keepdims=True)
    out_ref[...] = (acc_ref[...] / total).astype(jnp.bfloat16)


def attend(slot_mask, q_raw, q_gain, kv_tiles):
    rows, columns = q_raw.shape
    heads = columns // HD
    keys = kv_tiles[0].shape[2]
    slots = len(kv_tiles)
    kv_spec = pl.BlockSpec((2, None, keys, HD), lambda h, mask: (0, h, 0, 0))
    return pl.pallas_call(
        attend_kernel,
        grid_spec=pltpu.PrefetchScalarGridSpec(
            num_scalar_prefetch=1,
            grid=(heads,),
            in_specs=[
                pl.BlockSpec((rows, HD), lambda h, mask: (0, h)),
                pl.BlockSpec((1, HD), lambda h, mask: (0, 0)),
            ]
            + [kv_spec] * slots,
            out_specs=pl.BlockSpec((rows, HD), lambda h, mask: (0, h)),
            scratch_shapes=[
                pltpu.VMEM((slots, rows, keys), jnp.float32),
                pltpu.VMEM((rows, keys), jnp.float32),
                pltpu.VMEM((rows, keys), jnp.float32),
                pltpu.VMEM((rows, HD), jnp.float32),
            ],
        ),
        out_shape=jax.ShapeDtypeStruct((rows, columns), jnp.bfloat16),
    )(slot_mask, q_raw, q_gain.reshape(1, HD), *kv_tiles)


def on_device(tokens, w_qkv, q_gain, k_gain, w_out, neighbours, counts):
    tok_rows = tokens.shape[0]
    columns = w_qkv.shape[2]
    heads_here = columns // HD
    tiles_here = tok_rows // TILE
    total_tiles = neighbours.shape[0]
    feats = tokens.shape[1]
    mp_count = lax.axis_size("mp")
    mp_here = lax.axis_index("mp")

    def rows_of(block):
        return lax.dynamic_slice_in_dim(w_qkv, block * feats, feats, 0)

    projected = jnp.einsum(
        "tf,fjc->jtc", tokens, rows_of(mp_here), preferred_element_type=jnp.float32
    )
    for step in range(1, mp_count):
        source = (mp_here - step) % mp_count
        projected = projected + jnp.einsum(
            "tf,fjc->jtc",
            passed_along(tokens, "mp", step),
            rows_of(source),
            preferred_element_type=jnp.float32,
        )
    key_part = head_norm(projected[1], k_gain).transpose(1, 0, 2)
    value_part = projected[2].astype(jnp.bfloat16).reshape(tok_rows, heads_here, HD).transpose(1, 0, 2)
    paired = jnp.stack([key_part, value_part])
    position = lax.axis_index("seq")
    seq_count = lax.axis_size("seq")
    core = position % 2
    partner = [(source, source ^ 1) for source in range(seq_count)]
    from_m4 = passed_along(paired, "seq", 4)
    from_m2 = passed_along(paired, "seq", 2)
    from_p2 = passed_along(paired, "seq", -2)
    from_p4 = passed_along(paired, "seq", -4)
    fwd_own = lax.ppermute(paired, "seq", partner)
    fwd_a = lax.ppermute(from_m2, "seq", partner)
    fwd_b = lax.ppermute(from_p2, "seq", partner)
    fwd_c = lax.ppermute(jnp.where(core == 0, from_p4, from_m4), "seq", partner)
    kv_tiles = [paired, from_m4, from_m2, from_p2, from_p4, fwd_own, fwd_a, fwd_b, fwd_c]
    odd = core == 1
    slot_offsets = jnp.stack(
        [
            jnp.int32(0),
            jnp.int32(-4),
            jnp.int32(-2),
            jnp.int32(2),
            jnp.int32(4),
            jnp.where(odd, -1, 1).astype(jnp.int32),
            jnp.where(odd, -3, -1).astype(jnp.int32),
            jnp.where(odd, 1, 3).astype(jnp.int32),
            jnp.where(odd, 3, -3).astype(jnp.int32),
        ]
    )
    slot_tile = jnp.mod(position + slot_offsets, total_tiles)
    listed = lax.dynamic_slice_in_dim(neighbours, position, 1, 0)
    used_counts = lax.dynamic_slice_in_dim(counts, position, 1, 0)
    slot_used = jnp.arange(NB, dtype=jnp.int32)[None, :] < used_counts[:, None]
    hits = (listed[:, :, None] == slot_tile[None, None, :]) & slot_used[:, :, None]
    tile_mask = jnp.any(hits, axis=1)[0].astype(jnp.int32)
    q_raw = projected[0]
    attended = attend(tile_mask, q_raw, q_gain, kv_tiles)
    out_cols = w_out.shape[1] // mp_count
    terms = jnp.einsum(
        "tk,kjc->jtc",
        attended,
        w_out.reshape(w_out.shape[0], mp_count, out_cols),
        preferred_element_type=jnp.float32,
    ).astype(jnp.bfloat16)
    received = lax.all_to_all(terms, "mp", 0, 0, tiled=True).astype(jnp.float32)
    return jnp.sum(received, axis=0).astype(jnp.bfloat16)


def solution(mesh):
    return jax.shard_map(
        on_device,
        mesh=mesh,
        in_specs=(P("seq", "mp"), P(None, None, "mp"), P(), P(), P("mp", None), P(), P()),
        out_specs=P("seq", "mp"),
        check_vma=False,
    )
```

```python
import jax
import jax.numpy as jnp
from jax import lax
from jax.experimental import pallas as pl
from jax.experimental.pallas import tpu as pltpu
from jax.sharding import PartitionSpec as P

HD = 128
TILE = 384
REACH = 4
NB = 6


def passed_along(value, axis, steps):
    count = lax.axis_size(axis)
    pairs = [(source, (source + steps) % count) for source in range(count)]
    return lax.ppermute(value, axis, pairs)


def head_norm(projected, gain_vec):
    per_head = projected.reshape(projected.shape[0], -1, HD)
    factor = lax.rsqrt(jnp.mean(per_head * per_head, axis=-1, keepdims=True) + 1e-06)
    return (per_head * factor * gain_vec).astype(jnp.bfloat16)


def attend_kernel(mask_ref, q_ref, gain_ref, *rest):
    slots = len(rest) - 4
    kv_refs = rest[:slots]
    out_ref = rest[slots]
    m_ref, l_ref, acc_ref = rest[slots + 1 :]
    factor = HD ** (-0.5)
    q_raw = q_ref[...]
    norm = lax.rsqrt(jnp.mean(q_raw * q_raw, axis=-1, keepdims=True) + 1e-06)
    q = (q_raw * norm * gain_ref[...]).astype(jnp.bfloat16)
    m_ref[...] = jnp.full(m_ref.shape, -jnp.inf, jnp.float32)
    l_ref[...] = jnp.zeros(l_ref.shape, jnp.float32)
    acc_ref[...] = jnp.zeros(acc_ref.shape, jnp.float32)

    def scores_of(i):
        return lax.dot_general(
            q, kv_refs[i][0], (((1,), (1,)), ((), ())), preferred_element_type=jnp.float32
        )

    for i in range(slots):
        @pl.when(mask_ref[i] > 0)
        def _():
            m_ref[...] = jnp.maximum(m_ref[...], scores_of(i))
    highest = jnp.max(m_ref[...], axis=-1, keepdims=True)
    for i in range(slots):
        @pl.when(mask_ref[i] > 0)
        def _():
            p = jnp.exp((scores_of(i) - highest) * factor)
            l_ref[...] = l_ref[...] + p
            acc_ref[...] = acc_ref[...] + jnp.dot(
                p.astype(jnp.bfloat16), kv_refs[i][1], preferred_element_type=jnp.float32
            )
    total = jnp.sum(l_ref[...], axis=-1, keepdims=True)
    out_ref[...] = (acc_ref[...] / total).astype(jnp.bfloat16)


def attend(slot_mask, q_raw, q_gain, kv_tiles):
    rows, columns = q_raw.shape
    heads = columns // HD
    keys = kv_tiles[0].shape[2]
    slots = len(kv_tiles)
    kv_spec = pl.BlockSpec((2, None, keys, HD), lambda h, mask: (0, h, 0, 0))
    return pl.pallas_call(
        attend_kernel,
        grid_spec=pltpu.PrefetchScalarGridSpec(
            num_scalar_prefetch=1,
            grid=(heads,),
            in_specs=[
                pl.BlockSpec((rows, HD), lambda h, mask: (0, h)),
                pl.BlockSpec((1, HD), lambda h, mask: (0, 0)),
            ]
            + [kv_spec] * slots,
            out_specs=pl.BlockSpec((rows, HD), lambda h, mask: (0, h)),
            scratch_shapes=[
                pltpu.VMEM((rows, keys), jnp.float32),
                pltpu.VMEM((rows, keys), jnp.float32),
                pltpu.VMEM((rows, HD), jnp.float32),
            ],
        ),
        out_shape=jax.ShapeDtypeStruct((rows, columns), jnp.bfloat16),
    )(slot_mask, q_raw, q_gain.reshape(1, HD), *kv_tiles)


def on_device(tokens, w_qkv, q_gain, k_gain, w_out, neighbours, counts):
    tok_rows = tokens.shape[0]
    columns = w_qkv.shape[2]
    heads_here = columns // HD
    tiles_here = tok_rows // TILE
    total_tiles = neighbours.shape[0]
    feats = tokens.shape[1]
    mp_count = lax.axis_size("mp")
    mp_here = lax.axis_index("mp")

    def rows_of(block):
        return lax.dynamic_slice_in_dim(w_qkv, block * feats, feats, 0)

    position = lax.axis_index("seq")
    seq_count = lax.axis_size("seq")
    core = position % 2
    partner = [(source, source ^ 1) for source in range(seq_count)]

    def gathered_projection(part):
        projected = jnp.einsum(
            "tf,fjc->jtc", part, rows_of(mp_here), preferred_element_type=jnp.float32
        )
        for step in range(1, mp_count):
            source = (mp_here - step) % mp_count
            projected = projected + jnp.einsum(
                "tf,fjc->jtc",
                passed_along(part, "mp", step),
                rows_of(source),
                preferred_element_type=jnp.float32,
            )
        return projected

    def exchanged(paired):
        from_m4 = passed_along(paired, "seq", 4)
        from_m2 = passed_along(paired, "seq", 2)
        from_p2 = passed_along(paired, "seq", -2)
        from_p4 = passed_along(paired, "seq", -4)
        fwd_own = lax.ppermute(paired, "seq", partner)
        fwd_a = lax.ppermute(from_m2, "seq", partner)
        fwd_b = lax.ppermute(from_p2, "seq", partner)
        fwd_c = lax.ppermute(jnp.where(core == 0, from_p4, from_m4), "seq", partner)
        return [paired, from_m4, from_m2, from_p2, from_p4, fwd_own, fwd_a, fwd_b, fwd_c]

    half = tok_rows // 2
    kv_tiles = []
    query_parts = []
    later_rows = tokens[half:]
    for lower in (0, half):
        part = tokens[:half] if lower == 0 else later_rows
        projected = gathered_projection(part)
        key_part = head_norm(projected[1], k_gain).transpose(1, 0, 2)
        value_part = projected[2].astype(jnp.bfloat16).reshape(half, heads_here, HD).transpose(1, 0, 2)
        paired = jnp.stack([key_part, value_part])
        if lower == 0:
            paired, later_rows = lax.optimization_barrier((paired, later_rows))
        kv_tiles = kv_tiles + exchanged(paired)
        query_parts.append(projected[0])
    odd = core == 1
    slot_offsets = jnp.stack(
        [
            jnp.int32(0),
            jnp.int32(-4),
            jnp.int32(-2),
            jnp.int32(2),
            jnp.int32(4),
            jnp.where(odd, -1, 1).astype(jnp.int32),
            jnp.where(odd, -3, -1).astype(jnp.int32),
            jnp.where(odd, 1, 3).astype(jnp.int32),
            jnp.where(odd, 3, -3).astype(jnp.int32),
        ]
    )
    slot_tile = jnp.mod(position + slot_offsets, total_tiles)
    listed = lax.dynamic_slice_in_dim(neighbours, position, 1, 0)
    used_counts = lax.dynamic_slice_in_dim(counts, position, 1, 0)
    slot_used = jnp.arange(NB, dtype=jnp.int32)[None, :] < used_counts[:, None]
    hits = (listed[:, :, None] == slot_tile[None, None, :]) & slot_used[:, :, None]
    tile_mask = jnp.any(hits, axis=1)[0].astype(jnp.int32)
    tile_mask = jnp.concatenate([tile_mask, tile_mask])
    q_raw = jnp.concatenate(query_parts, axis=0)
    attended = attend(tile_mask, q_raw, q_gain, kv_tiles)
    out_cols = w_out.shape[1] // mp_count
    terms = jnp.einsum(
        "tk,kjc->jtc",
        attended,
        w_out.reshape(w_out.shape[0], mp_count, out_cols),
        preferred_element_type=jnp.float32,
    ).astype(jnp.bfloat16)
    received = lax.all_to_all(terms, "mp", 0, 0, tiled=True).astype(jnp.float32)
    return jnp.sum(received, axis=0).astype(jnp.bfloat16)


def solution(mesh):
    return jax.shard_map(
        on_device,
        mesh=mesh,
        in_specs=(P("seq", "mp"), P(None, None, "mp"), P(), P(), P("mp", None), P(), P()),
        out_specs=P("seq", "mp"),
        check_vma=False,
    )
```

```python
import jax
import jax.numpy as jnp
from jax import lax
from jax.experimental import pallas as pl
from jax.experimental.pallas import tpu as pltpu
from jax.sharding import PartitionSpec as P

HD = 128
TILE = 384
REACH = 4
NB = 6


def passed_along(value, axis, steps):
    count = lax.axis_size(axis)
    pairs = [(source, (source + steps) % count) for source in range(count)]
    return lax.ppermute(value, axis, pairs)


def head_norm(projected, gain_vec):
    per_head = projected.reshape(projected.shape[0], -1, HD)
    factor = lax.rsqrt(jnp.mean(per_head * per_head, axis=-1, keepdims=True) + 1e-06)
    return (per_head * factor * gain_vec).astype(jnp.bfloat16)


def attend_kernel(mask_ref, q_ref, gain_ref, *rest):
    slots = len(rest) - 4
    kv_refs = rest[:slots]
    out_ref = rest[slots]
    m_ref, l_ref, acc_ref = rest[slots + 1 :]
    factor = HD ** (-0.5)
    q_raw = q_ref[...]
    norm = lax.rsqrt(jnp.mean(q_raw * q_raw, axis=-1, keepdims=True) + 1e-06)
    q = (q_raw * norm * gain_ref[...] * factor).astype(jnp.bfloat16)
    m_ref[...] = jnp.full(m_ref.shape, -jnp.inf, jnp.float32)
    l_ref[...] = jnp.zeros(l_ref.shape, jnp.float32)
    acc_ref[...] = jnp.zeros(acc_ref.shape, jnp.float32)

    def scores_of(i):
        return lax.dot_general(
            q, kv_refs[i][0], (((1,), (1,)), ((), ())), preferred_element_type=jnp.float32
        )

    for i in range(slots):
        @pl.when(mask_ref[i] > 0)
        def _():
            m_ref[...] = jnp.maximum(m_ref[...], scores_of(i))
    highest = jnp.max(m_ref[...], axis=-1, keepdims=True)
    for i in range(slots):
        @pl.when(mask_ref[i] > 0)
        def _():
            p = jnp.exp(scores_of(i) - highest)
            l_ref[...] = l_ref[...] + p
            acc_ref[...] = acc_ref[...] + jnp.dot(
                p.astype(jnp.bfloat16), kv_refs[i][1], preferred_element_type=jnp.float32
            )
    total = jnp.sum(l_ref[...], axis=-1, keepdims=True)
    out_ref[...] = (acc_ref[...] / total).astype(jnp.bfloat16)


def attend(slot_mask, q_raw, q_gain, kv_tiles):
    rows, columns = q_raw.shape
    heads = columns // HD
    keys = kv_tiles[0].shape[2]
    slots = len(kv_tiles)
    kv_spec = pl.BlockSpec((2, None, keys, HD), lambda h, mask: (0, h, 0, 0))
    return pl.pallas_call(
        attend_kernel,
        grid_spec=pltpu.PrefetchScalarGridSpec(
            num_scalar_prefetch=1,
            grid=(heads,),
            in_specs=[
                pl.BlockSpec((rows, HD), lambda h, mask: (0, h)),
                pl.BlockSpec((1, HD), lambda h, mask: (0, 0)),
            ]
            + [kv_spec] * slots,
            out_specs=pl.BlockSpec((rows, HD), lambda h, mask: (0, h)),
            scratch_shapes=[
                pltpu.VMEM((rows, keys), jnp.float32),
                pltpu.VMEM((rows, keys), jnp.float32),
                pltpu.VMEM((rows, HD), jnp.float32),
            ],
        ),
        out_shape=jax.ShapeDtypeStruct((rows, columns), jnp.bfloat16),
    )(slot_mask, q_raw, q_gain.reshape(1, HD), *kv_tiles)


def on_device(tokens, w_qkv, q_gain, k_gain, w_out, neighbours, counts):
    tok_rows = tokens.shape[0]
    columns = w_qkv.shape[2]
    heads_here = columns // HD
    tiles_here = tok_rows // TILE
    total_tiles = neighbours.shape[0]
    feats = tokens.shape[1]
    mp_count = lax.axis_size("mp")
    mp_here = lax.axis_index("mp")

    def rows_of(block):
        return lax.dynamic_slice_in_dim(w_qkv, block * feats, feats, 0)

    projected = jnp.einsum(
        "tf,fjc->jtc", tokens, rows_of(mp_here), preferred_element_type=jnp.float32
    )
    for step in range(1, mp_count):
        source = (mp_here - step) % mp_count
        projected = projected + jnp.einsum(
            "tf,fjc->jtc",
            passed_along(tokens, "mp", step),
            rows_of(source),
            preferred_element_type=jnp.float32,
        )
    key_part = head_norm(projected[1], k_gain).transpose(1, 0, 2)
    value_part = projected[2].astype(jnp.bfloat16).reshape(tok_rows, heads_here, HD).transpose(1, 0, 2)
    paired = jnp.stack([key_part, value_part])
    position = lax.axis_index("seq")
    seq_count = lax.axis_size("seq")
    core = position % 2
    partner = [(source, source ^ 1) for source in range(seq_count)]
    from_m4 = passed_along(paired, "seq", 4)
    from_m2 = passed_along(paired, "seq", 2)
    from_p2 = passed_along(paired, "seq", -2)
    from_p4 = passed_along(paired, "seq", -4)
    fwd_own = lax.ppermute(paired, "seq", partner)
    fwd_a = lax.ppermute(from_m2, "seq", partner)
    fwd_b = lax.ppermute(from_p2, "seq", partner)
    fwd_c = lax.ppermute(jnp.where(core == 0, from_p4, from_m4), "seq", partner)
    kv_tiles = [paired, from_m4, from_m2, from_p2, from_p4, fwd_own, fwd_a, fwd_b, fwd_c]
    odd = core == 1
    slot_offsets = jnp.stack(
        [
            jnp.int32(0),
            jnp.int32(-4),
            jnp.int32(-2),
            jnp.int32(2),
            jnp.int32(4),
            jnp.where(odd, -1, 1).astype(jnp.int32),
            jnp.where(odd, -3, -1).astype(jnp.int32),
            jnp.where(odd, 1, 3).astype(jnp.int32),
            jnp.where(odd, 3, -3).astype(jnp.int32),
        ]
    )
    slot_tile = jnp.mod(position + slot_offsets, total_tiles)
    listed = lax.dynamic_slice_in_dim(neighbours, position, 1, 0)
    used_counts = lax.dynamic_slice_in_dim(counts, position, 1, 0)
    slot_used = jnp.arange(NB, dtype=jnp.int32)[None, :] < used_counts[:, None]
    hits = (listed[:, :, None] == slot_tile[None, None, :]) & slot_used[:, :, None]
    tile_mask = jnp.any(hits, axis=1)[0].astype(jnp.int32)
    q_raw = projected[0]
    attended = attend(tile_mask, q_raw, q_gain, kv_tiles)
    out_cols = w_out.shape[1] // mp_count
    terms = jnp.einsum(
        "tk,kjc->jtc",
        attended,
        w_out.reshape(w_out.shape[0], mp_count, out_cols),
        preferred_element_type=jnp.float32,
    ).astype(jnp.bfloat16)
    received = lax.all_to_all(terms, "mp", 0, 0, tiled=True).astype(jnp.float32)
    return jnp.sum(received, axis=0).astype(jnp.bfloat16)


def solution(mesh):
    return jax.shard_map(
        on_device,
        mesh=mesh,
        in_specs=(P("seq", "mp"), P(None, None, "mp"), P(), P(), P("mp", None), P(), P()),
        out_specs=P("seq", "mp"),
        check_vma=False,
    )
```

```python
import jax
import jax.numpy as jnp
from jax import lax
from jax.experimental import pallas as pl
from jax.experimental.pallas import tpu as pltpu
from jax.sharding import PartitionSpec as P

HD = 128
TILE = 384
REACH = 4
NB = 6


def passed_along(value, axis, steps):
    count = lax.axis_size(axis)
    pairs = [(source, (source + steps) % count) for source in range(count)]
    return lax.ppermute(value, axis, pairs)


def head_norm(projected, gain_vec):
    per_head = projected.reshape(projected.shape[0], -1, HD)
    factor = lax.rsqrt(jnp.mean(per_head * per_head, axis=-1, keepdims=True) + 1e-06)
    return (per_head * factor * gain_vec).astype(jnp.bfloat16)


def attend_kernel(mask_ref, q_ref, gain_ref, *rest):
    slots = len(rest) - 4
    kv_refs = rest[:slots]
    out_ref = rest[slots]
    m_ref, l_ref, acc_ref = rest[slots + 1 :]
    factor = HD ** (-0.5)
    q_raw = q_ref[...]
    norm = lax.rsqrt(jnp.mean(q_raw * q_raw, axis=-1, keepdims=True) + 1e-06)
    q = (q_raw * norm * gain_ref[...]).astype(jnp.bfloat16)
    m_ref[...] = jnp.full(m_ref.shape, -jnp.inf, jnp.float32)
    l_ref[...] = jnp.zeros(l_ref.shape, jnp.float32)
    acc_ref[...] = jnp.zeros(acc_ref.shape, jnp.float32)

    def scores_of(i):
        return lax.dot_general(
            q, kv_refs[i][0], (((1,), (1,)), ((), ())), preferred_element_type=jnp.float32
        )

    for i in range(slots):
        @pl.when(mask_ref[i] > 0)
        def _():
            m_ref[...] = jnp.maximum(m_ref[...], scores_of(i))
    highest = jnp.max(m_ref[...], axis=-1, keepdims=True)
    for i in range(slots):
        @pl.when(mask_ref[i] > 0)
        def _():
            p = jnp.exp((scores_of(i) - highest) * factor)
            l_ref[...] = l_ref[...] + p
            acc_ref[...] = acc_ref[...] + jnp.dot(
                p.astype(jnp.bfloat16), kv_refs[i][1], preferred_element_type=jnp.float32
            )
    total = jnp.sum(l_ref[...], axis=-1, keepdims=True)
    out_ref[...] = (acc_ref[...] / total).astype(jnp.bfloat16)


def attend(slot_mask, q_raw, q_gain, kv_tiles):
    rows, columns = q_raw.shape
    heads = columns // HD
    keys = kv_tiles[0].shape[2]
    slots = len(kv_tiles)
    kv_spec = pl.BlockSpec((2, None, keys, HD), lambda h, mask: (0, h, 0, 0))
    return pl.pallas_call(
        attend_kernel,
        grid_spec=pltpu.PrefetchScalarGridSpec(
            num_scalar_prefetch=1,
            grid=(heads,),
            in_specs=[
                pl.BlockSpec((rows, HD), lambda h, mask: (0, h)),
                pl.BlockSpec((1, HD), lambda h, mask: (0, 0)),
            ]
            + [kv_spec] * slots,
            out_specs=pl.BlockSpec((rows, HD), lambda h, mask: (0, h)),
            scratch_shapes=[
                pltpu.VMEM((rows, keys), jnp.float32),
                pltpu.VMEM((rows, keys), jnp.float32),
                pltpu.VMEM((rows, HD), jnp.float32),
            ],
        ),
        out_shape=jax.ShapeDtypeStruct((rows, columns), jnp.bfloat16),
    )(slot_mask, q_raw, q_gain.reshape(1, HD), *kv_tiles)


def on_device(tokens, w_qkv, q_gain, k_gain, w_out, neighbours, counts):
    tok_rows = tokens.shape[0]
    columns = w_qkv.shape[2]
    heads_here = columns // HD
    tiles_here = tok_rows // TILE
    total_tiles = neighbours.shape[0]
    feats = tokens.shape[1]
    mp_count = lax.axis_size("mp")
    mp_here = lax.axis_index("mp")

    def rows_of(block):
        return lax.dynamic_slice_in_dim(w_qkv, block * feats, feats, 0)

    projected = jnp.einsum(
        "tf,fjc->jtc", tokens, rows_of(mp_here), preferred_element_type=jnp.float32
    )
    for step in range(1, mp_count):
        source = (mp_here - step) % mp_count
        projected = projected + jnp.einsum(
            "tf,fjc->jtc",
            passed_along(tokens, "mp", step),
            rows_of(source),
            preferred_element_type=jnp.float32,
        )
    key_part = head_norm(projected[1], k_gain).transpose(1, 0, 2)
    value_part = projected[2].astype(jnp.bfloat16).reshape(tok_rows, heads_here, HD).transpose(1, 0, 2)
    paired = jnp.stack([key_part, value_part])
    position = lax.axis_index("seq")
    seq_count = lax.axis_size("seq")
    core = position % 2
    partner = [(source, source ^ 1) for source in range(seq_count)]
    from_m4 = passed_along(paired, "seq", 4)
    from_m2 = passed_along(paired, "seq", 2)
    from_p2 = passed_along(paired, "seq", -2)
    from_p4 = passed_along(paired, "seq", -4)
    fwd_own = lax.ppermute(paired, "seq", partner)
    fwd_a = lax.ppermute(from_m2, "seq", partner)
    fwd_b = lax.ppermute(from_p2, "seq", partner)
    fwd_even = lax.ppermute(from_m4, "seq", [(s, s ^ 1) for s in range(1, seq_count, 2)])
    fwd_odd = lax.ppermute(from_p4, "seq", [(s, s ^ 1) for s in range(0, seq_count, 2)])
    kv_tiles = [paired, from_m4, from_m2, from_p2, from_p4, fwd_own, fwd_a, fwd_b, fwd_even, fwd_odd]
    odd = core == 1
    slot_offsets = jnp.stack(
        [
            jnp.int32(0),
            jnp.int32(-4),
            jnp.int32(-2),
            jnp.int32(2),
            jnp.int32(4),
            jnp.where(odd, -1, 1).astype(jnp.int32),
            jnp.where(odd, -3, -1).astype(jnp.int32),
            jnp.where(odd, 1, 3).astype(jnp.int32),
            jnp.int32(-3),
            jnp.int32(3),
        ]
    )
    slot_tile = jnp.mod(position + slot_offsets, total_tiles)
    slot_tile = slot_tile.at[8].set(jnp.where(odd, -1, slot_tile[8]))
    slot_tile = slot_tile.at[9].set(jnp.where(odd, slot_tile[9], -1))
    listed = lax.dynamic_slice_in_dim(neighbours, position, 1, 0)
    used_counts = lax.dynamic_slice_in_dim(counts, position, 1, 0)
    slot_used = jnp.arange(NB, dtype=jnp.int32)[None, :] < used_counts[:, None]
    hits = (listed[:, :, None] == slot_tile[None, None, :]) & slot_used[:, :, None]
    tile_mask = jnp.any(hits, axis=1)[0].astype(jnp.int32)
    q_raw = projected[0]
    attended = attend(tile_mask, q_raw, q_gain, kv_tiles)
    out_cols = w_out.shape[1] // mp_count
    terms = jnp.einsum(
        "tk,kjc->jtc",
        attended,
        w_out.reshape(w_out.shape[0], mp_count, out_cols),
        preferred_element_type=jnp.float32,
    ).astype(jnp.bfloat16)
    received = lax.all_to_all(terms, "mp", 0, 0, tiled=True).astype(jnp.float32)
    return jnp.sum(received, axis=0).astype(jnp.bfloat16)


def solution(mesh):
    return jax.shard_map(
        on_device,
        mesh=mesh,
        in_specs=(P("seq", "mp"), P(None, None, "mp"), P(), P(), P("mp", None), P(), P()),
        out_specs=P("seq", "mp"),
        check_vma=False,
    )
```
